128 devices in a mesh: blk: 16 (over x, y_hi, core), req: 8 (over y_lo, z).
Axes of the slice: x: 4, y: 4 (y_hi: 2, y_lo: 2; y = y_hi * 2 + y_lo), z: 4, core: 2. Of those that a mesh axis runs over, the one named last changes fastest.
Arguments:
- long_q: bfloat16 [16384, 2048], P('blk', 'req'), may hold values from -6 to 6
- long_k: bfloat16 [16384, 2048], P('blk', 'req'), may hold values from -6 to 6
- long_v: bfloat16 [16384, 2048], P('blk', 'req'), may hold values from -6 to 6
- short_q: bfloat16 [8192, 2048], P('blk', 'req'), may hold values from -6 to 6
- short_k: bfloat16 [8192, 2048], P('blk', 'req'), may hold values from -6 to 6
- short_v: bfloat16 [8192, 2048], P('blk', 'req'), may hold values from -6 to 6
- short_seg: int32 [16, 512], P('blk'), may hold values from 0 to 15, never falling along the last dimension, each value on 1 to 96 neighbouring positions
- pool_kv: bfloat16 [1024, 2, 16, 2048], P('blk', None, None, 'req'), may hold values from -6 to 6
- page_table: int32 [16, 16, 4], replicated, may hold values from 0 to 1023, as said below
- w_out: bfloat16 [2048, 2048], replicated, may hold values from -0.125 to 0.125
Outputs:
- long_out: bfloat16 [16384, 2048], P(('blk', 'req'))
- short_out: bfloat16 [8192, 2048], P(('blk', 'req'))
The draws below stay inside these ranges and needn't reach their ends.
Inputs may be any that keep to these rules, and one draw needn't show every extreme that they name: `short_seg`: along each pack the request numbers never fall, and each of the 16 requests has 1 to 96 tokens, one of them exactly 96. `page_table`: entry [b, s, j] is o * 64 + i for page i of the pool rows held by index o of blk; for every pack b and every o exactly 4 of the 64 entries of b name pages of o.
All inputs are finite; a program needn't handle non-finite values.
Results may differ from the reference program's by a relative error of at most 0.015.
Values may be sent and summed in bfloat16 or wider, within the bound.
No kernel may reach another device: no remote copies, remote signals or barrier semaphores. Data moves between devices by JAX's collectives and lax.ppermute only.
A program may use at most 128 MiB of HBM per device.

```python
import math
import jax
import jax.numpy as jnp
import numpy as np
from jax import lax

D = 2048
HEADS = 16
HD = 128
PACK = 512
SEGS = 16
SMAX = 96
PPS = 4
PAGE = 16
POOL = 64
LONG = 16384
QW = 2048
SHORT_ROWS = 8192
CAP = 4
N_BLK = 16


def paired(key, row_count):
    key_query, key_keys = jax.random.split(key, 2)
    queries = jnp.clip(1.6 * jax.random.normal(key_query, (row_count, QW), jnp.float32), -6.0, 6.0)
    keys_all = jnp.clip(1.6 * jax.random.normal(key_keys, (row_count, QW), jnp.float32), -6.0, 6.0)
    return (queries, keys_all)


def draw_long_q(key, part):
    return paired(jax.random.fold_in(key, 11), LONG)[0].astype(jnp.bfloat16)


def draw_long_k(key, part):
    return paired(jax.random.fold_in(key, 11), LONG)[1].astype(jnp.bfloat16)


def draw_short_q(key, part):
    return paired(jax.random.fold_in(key, 23), SHORT_ROWS)[0].astype(jnp.bfloat16)


def draw_short_k(key, part):
    return paired(jax.random.fold_in(key, 23), SHORT_ROWS)[1].astype(jnp.bfloat16)


def draw_page_table(key, part):
    entries = SEGS * PPS
    blocks = entries // CAP
    key_perm, key_local = jax.random.split(jax.random.fold_in(key, 37))
    repeated = jnp.tile(jnp.arange(blocks, dtype=jnp.int32), CAP)
    owners = jax.vmap(lambda one_key: jax.random.permutation(one_key, repeated))(jax.random.split(key_perm, blocks))
    places = jax.random.randint(key_local, (blocks, entries), 0, POOL, dtype=jnp.int32)
    is_last = owners[0] == blocks - 1
    first_last = is_last & (jnp.cumsum(is_last.astype(jnp.int32)) == 1)
    is_first = owners[0] == 0
    first_first = is_first & (jnp.cumsum(is_first.astype(jnp.int32)) == 1)
    row_zero = jnp.where(first_last, POOL - 1, jnp.where(first_first, 0, places[0]))
    places = places.at[0].set(row_zero)
    return (owners * POOL + places).reshape(blocks, SEGS, PPS).astype(jnp.int32)


def levels(rng, dims, cuts, least, largest):
    gain = 1.0
    for axis_at, parts in cuts:
        heights = jax.random.uniform(jax.random.fold_in(jax.random.fold_in(rng, 6), axis_at), (parts,), jnp.float32, least / len(cuts), largest / len(cuts))
        gain = gain * jnp.repeat(jnp.exp(heights), dims[axis_at] // parts).reshape((-1,) + (1,) * (len(dims) - 1 - axis_at))
    return gain


def split_up(count, total, most, slope):
    portions = [(1 << 20) // math.isqrt(grade ** slope) + 1 for grade in range(2, count + 1)]
    rest, given = total - most - (count - 1), [1] * (count - 1)
    while rest > 0:
        free = [i for i in range(count - 1) if given[i] < most]
        whole, left = sum([portions[i] for i in free]), rest
        for i in free:
            extra = min(most - given[i], max(1, left * portions[i] // whole), rest)
            given[i] = given[i] + extra
            rest = rest - extra
    return np.array([most] + given)


def uneven(own_key, count, total, bound, slope):
    if count == 2:
        one = jax.random.randint(own_key, (), max(1, total - bound), min(bound, total - 1) + 1)
        return jnp.stack([one, total - one])
    tallies = jnp.asarray(split_up(count, total, bound, slope), jnp.int32)
    twos = (count - 1) // 2
    source_of, receiver = tallies[1:1 + 2 * twos:2], tallies[2:2 + 2 * twos:2]
    slack = jnp.minimum(source_of - 1, bound - receiver)
    moved = jax.random.randint(jax.random.fold_in(own_key, 1), (twos,), 0, 1 << 20) % (slack + 1)
    tallies = tallies.at[1:1 + 2 * twos:2].set(source_of - moved).at[2:2 + 2 * twos:2].set(receiver + moved)
    return tallies[jax.random.permutation(jax.random.fold_in(own_key, 2), count)]


def centred(own_key, dims, deviation, most, cuts=(), kind=jnp.bfloat16):
    values = deviation * jax.random.normal(own_key, dims, jnp.float32)
    if cuts:
        values = values * levels(own_key, dims, cuts, -0.22, 0.18)
    return jnp.clip(values, -most, most).astype(kind)


def setup_inputs(seed: int = 0) -> dict:
    arg_keys = jax.random.split(jax.random.key(seed), 11)
    return {
        "long_q": draw_long_q(jax.random.fold_in(arg_keys[10], 71), 0),
        "long_k": draw_long_k(jax.random.fold_in(arg_keys[10], 71), 0),
        "long_v": centred(arg_keys[2], (LONG, QW), 1.0, 6.0, ((0, 16), (1, 8))),
        "short_q": draw_short_q(jax.random.fold_in(arg_keys[10], 71), 0),
        "short_k": draw_short_k(jax.random.fold_in(arg_keys[10], 71), 0),
        "short_v": centred(arg_keys[5], (SHORT_ROWS, QW), 1.0, 6.0, ((0, 16), (1, 8))),
        "short_seg": jax.vmap(lambda own: jnp.searchsorted(jnp.cumsum(uneven(own, SEGS, PACK, SMAX, 2)), jnp.arange(PACK), side="right"))(jax.random.split(arg_keys[6], N_BLK)).reshape((N_BLK, PACK)).astype(jnp.int32),
        "pool_kv": centred(arg_keys[7], (N_BLK * POOL, 2, PAGE, QW), 1.6, 6.0, ((0, 16), (3, 8))),
        "page_table": draw_page_table(jax.random.fold_in(arg_keys[10], 71), 0),
        "w_out": centred(arg_keys[9], (QW, D), QW ** -0.5, 0.125),
    }


very_negative = -1e30


def reference(long_q, long_k, long_v, short_q, short_k, short_v, short_seg, pool_kv, page_table, w_out):
    scale = HD ** -0.5
    block_rows = math.gcd(LONG, 1024)
    block_count = LONG // block_rows
    query_heads = long_q.reshape(block_count, block_rows, HEADS, HD)
    key_heads = long_k.reshape(block_count, block_rows, HEADS, HD)
    value_heads = long_v.reshape(block_count, block_rows, HEADS, HD)

    def query_block(block_num):
        queries = lax.dynamic_index_in_dim(query_heads, block_num, 0, keepdims=False).astype(jnp.float32)
        query_pos = block_num * block_rows + jnp.arange(block_rows, dtype=jnp.int32)

        def key_step(key_num, state_now):
            acc_sum, run_max, run_total = state_now
            keys_now = lax.dynamic_index_in_dim(key_heads, key_num, 0, keepdims=False).astype(jnp.float32)
            values_now = lax.dynamic_index_in_dim(value_heads, key_num, 0, keepdims=False).astype(jnp.float32)
            scores = jnp.einsum("qhd,khd->hqk", queries, keys_now) * scale
            key_pos = key_num * block_rows + jnp.arange(block_rows, dtype=jnp.int32)
            allowed = (key_pos[None, :] <= query_pos[:, None])[None]
            scores = jnp.where(allowed, scores, very_negative)
            new_max = jnp.maximum(run_max, jnp.max(scores, axis=-1))
            weights = jnp.where(allowed, jnp.exp(scores - new_max[..., None]), 0.0)
            factor = jnp.exp(run_max - new_max)
            run_total = run_total * factor + jnp.sum(weights, axis=-1)
            rounded = weights.astype(jnp.bfloat16).astype(jnp.float32)
            acc_sum = acc_sum * factor[..., None] + jnp.einsum("hqk,khd->hqd", rounded, values_now)
            return acc_sum, new_max, run_total

        init = (jnp.zeros((HEADS, block_rows, HD), jnp.float32),
                jnp.full((HEADS, block_rows), very_negative, jnp.float32),
                jnp.zeros((HEADS, block_rows), jnp.float32))
        acc_sum, run_max, run_total = lax.fori_loop(jnp.int32(0), block_num + 1, key_step, init)
        merged = acc_sum / run_total[..., None]
        return merged.transpose(1, 0, 2).reshape(block_rows, QW).astype(jnp.bfloat16)

    long_attn = lax.map(query_block, jnp.arange(block_count, dtype=jnp.int32)).reshape(LONG, QW)

    cache_len = SEGS * PPS * PAGE

    def pack_block(block_num):
        page_rows = lax.dynamic_index_in_dim(page_table, block_num, 0, keepdims=False).reshape(SEGS * PPS)
        fetched = pool_kv[page_rows]
        cache_keys = fetched[:, 0].reshape(cache_len, QW)
        cache_values = fetched[:, 1].reshape(cache_len, QW)
        first_row = (block_num * PACK).astype(jnp.int32)
        queries = lax.dynamic_slice_in_dim(short_q, first_row, PACK, 0)
        keys_new = lax.dynamic_slice_in_dim(short_k, first_row, PACK, 0)
        values_new = lax.dynamic_slice_in_dim(short_v, first_row, PACK, 0)
        segment = lax.dynamic_index_in_dim(short_seg, block_num, 0, keepdims=False)
        key_rows = jnp.concatenate([cache_keys, keys_new], 0).astype(jnp.float32).reshape(cache_len + PACK, HEADS, HD)
        value_rows = jnp.concatenate([cache_values, values_new], 0).astype(jnp.float32).reshape(cache_len + PACK, HEADS, HD)
        query_rows = queries.astype(jnp.float32).reshape(PACK, HEADS, HD)
        positions = jnp.arange(PACK, dtype=jnp.int32)
        key_seg = jnp.concatenate([jnp.arange(cache_len, dtype=jnp.int32) // (PPS * PAGE), segment.astype(jnp.int32)])
        key_pos = jnp.concatenate([jnp.full((cache_len,), -1, jnp.int32), positions])
        allowed = ((key_seg[None, :] == segment[:, None]) & (key_pos[None, :] <= positions[:, None]))[None]
        scores = jnp.einsum("qhd,khd->hqk", query_rows, key_rows) * scale
        scores = jnp.where(allowed, scores, very_negative)
        row_max = jnp.max(scores, axis=-1)
        weights = jnp.where(allowed, jnp.exp(scores - row_max[..., None]), 0.0)
        total = jnp.sum(weights, axis=-1)
        rounded = weights.astype(jnp.bfloat16).astype(jnp.float32)
        numer = jnp.einsum("hqk,khd->hqd", rounded, value_rows)
        merged = numer / total[..., None]
        return merged.transpose(1, 0, 2).reshape(PACK, QW).astype(jnp.bfloat16)

    short_attn = lax.map(pack_block, jnp.arange(N_BLK, dtype=jnp.int32)).reshape(N_BLK * PACK, QW)
    long_out = jnp.dot(long_attn, w_out, preferred_element_type=jnp.float32).astype(jnp.bfloat16)
    short_out = jnp.dot(short_attn, w_out, preferred_element_type=jnp.float32).astype(jnp.bfloat16)
    return long_out, short_out
```

```python
import math

import jax
import jax.numpy as jnp
from jax import lax
from jax.sharding import PartitionSpec as P

HD = 128
PPS = 4


very_negative = -1e30


def fold_block(state_now, query_heads, query_pos, key_block, value_block, block_first):
    acc_sum, run_max, run_total = state_now
    heads_dev = query_heads.shape[1]
    key_heads = key_block.reshape(key_block.shape[0], heads_dev, HD)
    value_heads = value_block.reshape(value_block.shape[0], heads_dev, HD)
    scores = jnp.einsum(
        "qhd,khd->hqk", query_heads, key_heads, preferred_element_type=jnp.float32
    ) * HD ** (-0.5)
    key_pos = block_first + jnp.arange(key_block.shape[0], dtype=jnp.int32)
    allowed = (key_pos[None, :] <= query_pos[:, None])[None]
    scores = jnp.where(allowed, scores, very_negative)
    new_max = jnp.maximum(run_max, jnp.max(scores, axis=-1))
    weights = jnp.where(allowed, jnp.exp(scores - new_max[..., None]), 0.0)
    factor = jnp.exp(run_max - new_max)
    run_total = run_total * factor + jnp.sum(weights, axis=-1)
    acc_sum = acc_sum * factor[..., None] + jnp.einsum(
        "hqk,khd->hqd",
        weights.astype(jnp.bfloat16),
        value_heads,
        preferred_element_type=jnp.float32,
    )
    return (acc_sum, new_max, run_total)


def prompt_attention(queries, query_pos, long_k, long_v):
    row_count, width = queries.shape
    heads_dev = width // HD
    query_heads = queries.reshape(row_count, heads_dev, HD)
    last_pos = jnp.max(query_pos)
    init = (
        jnp.zeros((heads_dev, row_count, HD), jnp.float32),
        jnp.full((heads_dev, row_count), very_negative, jnp.float32),
        jnp.zeros((heads_dev, row_count), jnp.float32),
    )
    key_piece = lax.all_gather(long_k, "blk", axis=0, tiled=True)
    value_piece = lax.all_gather(long_v, "blk", axis=0, tiled=True)
    piece_rows = key_piece.shape[0]
    step_rows = math.gcd(piece_rows, 1024)

    def one_step(block_num, state_in):
        block_start = block_num * step_rows
        key_block = lax.dynamic_slice_in_dim(key_piece, block_start, step_rows, 0)
        value_block = lax.dynamic_slice_in_dim(value_piece, block_start, step_rows, 0)

        def compute_block(state_live):
            return fold_block(
                state_live, query_heads, query_pos, key_block, value_block, block_start
            )

        def keep_state(state_skip):
            return state_skip

        return lax.cond(block_start <= last_pos, compute_block, keep_state, state_in)

    acc_sum, run_max, run_total = lax.fori_loop(0, piece_rows // step_rows, one_step, init)
    merged = acc_sum / run_total[..., None]
    return merged.transpose(1, 0, 2).reshape(row_count, width).astype(jnp.bfloat16)


def pack_attention(
    short_q, short_k, short_v, short_seg, pool_kv, page_table, block_index, block_count
):
    pack_rows, width = short_q.shape
    heads_dev = width // HD
    pool_pages = pool_kv.shape[0]
    page_len = pool_kv.shape[2]
    page_rows = page_table.reshape(block_count, -1)
    entries = page_rows.shape[1]
    capacity = entries // block_count
    owners = page_rows // pool_pages
    places = page_rows % pool_pages
    wanted = owners == block_index
    ranks = jnp.cumsum(wanted.astype(jnp.int32), axis=1) - 1
    picked = wanted[:, :, None] & (
        ranks[:, :, None] == jnp.arange(capacity, dtype=jnp.int32)[None, None, :]
    )
    send_places = jnp.sum(jnp.where(picked, places[:, :, None], 0), axis=1)
    outgoing = pool_kv[send_places.reshape(-1)].reshape(block_count, capacity, 2, page_len, width)
    arrived = lax.all_to_all(outgoing, "blk", split_axis=0, concat_axis=0, tiled=True)
    my_owners = lax.dynamic_index_in_dim(owners, block_index, 0, keepdims=False)
    order = jnp.arange(entries, dtype=jnp.int32)
    before = (my_owners[None, :] == my_owners[:, None]) & (order[None, :] < order[:, None])
    slots = my_owners * capacity + jnp.sum(before.astype(jnp.int32), axis=1)
    fetched = arrived.reshape(block_count * capacity, 2, page_len, width)[slots]
    cache_len = entries * page_len
    key_rows = jnp.concatenate([fetched[:, 0].reshape(cache_len, width), short_k], 0)
    value_rows = jnp.concatenate([fetched[:, 1].reshape(cache_len, width), short_v], 0)
    segment = short_seg[0]
    positions = jnp.arange(pack_rows, dtype=jnp.int32)
    key_seg = jnp.concatenate([jnp.arange(cache_len, dtype=jnp.int32) // (PPS * page_len), segment])
    key_pos = jnp.concatenate([jnp.full((cache_len,), -1, jnp.int32), positions])
    allowed = ((key_seg[None, :] == segment[:, None]) & (key_pos[None, :] <= positions[:, None]))[
        None
    ]
    query_heads = short_q.reshape(pack_rows, heads_dev, HD)
    key_heads = key_rows.reshape(cache_len + pack_rows, heads_dev, HD)
    value_heads = value_rows.reshape(cache_len + pack_rows, heads_dev, HD)
    scores = jnp.einsum(
        "qhd,khd->hqk", query_heads, key_heads, preferred_element_type=jnp.float32
    ) * HD ** (-0.5)
    scores = jnp.where(allowed, scores, very_negative)
    row_max = jnp.max(scores, axis=-1)
    weights = jnp.where(allowed, jnp.exp(scores - row_max[..., None]), 0.0)
    total = jnp.sum(weights, axis=-1)
    numer = jnp.einsum(
        "hqk,khd->hqd",
        weights.astype(jnp.bfloat16),
        value_heads,
        preferred_element_type=jnp.float32,
    )
    merged = numer / total[..., None]
    return merged.transpose(1, 0, 2).reshape(pack_rows, width).astype(jnp.bfloat16)


def per_device(
    long_q, long_k, long_v, short_q, short_k, short_v, short_seg, pool_kv, page_table, w_out
):
    block_count = lax.axis_size("blk")
    block_index = lax.axis_index("blk")
    row_count, width = long_q.shape
    query_pos = block_index * row_count + jnp.arange(row_count, dtype=jnp.int32)
    long_attn = prompt_attention(long_q, query_pos, long_k, long_v)
    short_attn = pack_attention(
        short_q, short_k, short_v, short_seg, pool_kv, page_table, block_index, block_count
    )
    long_rows = lax.all_to_all(long_attn, "req", 0, 1, tiled=True)
    short_rows = lax.all_to_all(short_attn, "req", 0, 1, tiled=True)
    long_out = jnp.dot(long_rows, w_out, preferred_element_type=jnp.float32).astype(jnp.bfloat16)
    short_out = jnp.dot(short_rows, w_out, preferred_element_type=jnp.float32).astype(jnp.bfloat16)
    return (long_out, short_out)


def solution(mesh):
    placed = (
        P("blk", "req"),
        P("blk", "req"),
        P("blk", "req"),
        P("blk", "req"),
        P("blk", "req"),
        P("blk", "req"),
        P("blk", None),
        P("blk", None, None, "req"),
        P(),
        P(),
    )
    return jax.shard_map(
        per_device,
        mesh=mesh,
        in_specs=placed,
        out_specs=(P(("blk", "req"), None), P(("blk", "req"), None)),
        check_vma=False,
    )
```

```python
import functools
import math

import jax
import jax.numpy as jnp
from jax import lax
from jax.experimental import pallas as pl
from jax.experimental.pallas import tpu as pltpu
from jax.sharding import PartitionSpec as P

HD = 128
PPS = 4


very_negative = -1e30


def flash_body(blk_ref, q_ref, k_ref, v_ref, o_ref, m_sc, l_sc, acc_sc, *, heads, tq, tk, q_rows):
    q_tile = pl.program_id(0)
    k_tile = pl.program_id(1)
    first_query = blk_ref[0] * q_rows + q_tile * tq
    last_tile = (first_query + tq - 1) // tk

    @pl.when(k_tile == 0)
    def _():
        m_sc[...] = jnp.full(m_sc.shape, very_negative, jnp.float32)
        l_sc[...] = jnp.zeros(l_sc.shape, jnp.float32)
        acc_sc[...] = jnp.zeros(acc_sc.shape, jnp.float32)

    def fold(masked):
        for h in range(heads):
            cols = slice(h * HD, (h + 1) * HD)
            scores = lax.dot_general(
                q_ref[:, cols], k_ref[:, cols], (((1,), (1,)), ((), ())),
                preferred_element_type=jnp.float32,
            ) * HD ** (-0.5)
            if masked:
                query_pos = first_query + lax.broadcasted_iota(jnp.int32, (tq, tk), 0)
                key_pos = k_tile * tk + lax.broadcasted_iota(jnp.int32, (tq, tk), 1)
                scores = jnp.where(key_pos <= query_pos, scores, very_negative)
            run_max = m_sc[h]
            new_max = jnp.maximum(run_max, jnp.max(scores, axis=1, keepdims=True))
            weights = jnp.exp(scores - new_max[:, :1])
            factor = jnp.exp(run_max - new_max)
            l_sc[h] = l_sc[h] * factor + jnp.sum(weights, axis=1, keepdims=True)
            m_sc[h] = new_max
            acc_sc[h] = acc_sc[h] * factor + jnp.dot(
                weights.astype(jnp.bfloat16), v_ref[:, cols], preferred_element_type=jnp.float32
            )

    needs_mask = (k_tile + 1) * tk - 1 > first_query

    @pl.when((k_tile <= last_tile) & jnp.logical_not(needs_mask))
    def _():
        fold(False)

    @pl.when((k_tile <= last_tile) & needs_mask)
    def _():
        fold(True)

    @pl.when(k_tile == last_tile)
    def _():
        for h in range(heads):
            o_ref[:, h * HD:(h + 1) * HD] = (acc_sc[h] / l_sc[h]).astype(o_ref.dtype)


def prompt_attention(queries, block_index, long_k, long_v):
    row_count, width = queries.shape
    heads_dev = width // HD
    key_piece = lax.all_gather(long_k, "blk", axis=0, tiled=True)
    value_piece = lax.all_gather(long_v, "blk", axis=0, tiled=True)
    piece_rows = key_piece.shape[0]
    tq = min(row_count, 512)
    tk = min(row_count, 1024)

    def kv_map(q_tile, k_tile, blk_ref):
        last_tile = (blk_ref[0] * row_count + q_tile * tq + tq - 1) // tk
        return (jnp.minimum(k_tile, last_tile), 0)

    body = functools.partial(flash_body, heads=heads_dev, tq=tq, tk=tk, q_rows=row_count)
    return pl.pallas_call(
        body,
        out_shape=jax.ShapeDtypeStruct((row_count, width), jnp.bfloat16),
        grid_spec=pltpu.PrefetchScalarGridSpec(
            num_scalar_prefetch=1,
            grid=(row_count // tq, piece_rows // tk),
            in_specs=[
                pl.BlockSpec((tq, width), lambda q_tile, k_tile, blk_ref: (q_tile, 0)),
                pl.BlockSpec((tk, width), kv_map),
                pl.BlockSpec((tk, width), kv_map),
            ],
            out_specs=pl.BlockSpec((tq, width), lambda q_tile, k_tile, blk_ref: (q_tile, 0)),
            scratch_shapes=[
                pltpu.VMEM((heads_dev, tq, HD), jnp.float32),
                pltpu.VMEM((heads_dev, tq, HD), jnp.float32),
                pltpu.VMEM((heads_dev, tq, HD), jnp.float32),
            ],
        ),
        compiler_params=pltpu.CompilerParams(dimension_semantics=("arbitrary", "arbitrary")),
    )(jnp.reshape(block_index, (1,)).astype(jnp.int32), queries, key_piece, value_piece)


def pack_attention(
    short_q, short_k, short_v, short_seg, pool_kv, page_table, block_index, block_count
):
    pack_rows, width = short_q.shape
    heads_dev = width // HD
    pool_pages = pool_kv.shape[0]
    page_len = pool_kv.shape[2]
    page_rows = page_table.reshape(block_count, -1)
    entries = page_rows.shape[1]
    capacity = entries // block_count
    owners = page_rows // pool_pages
    places = page_rows % pool_pages
    wanted = owners == block_index
    ranks = jnp.cumsum(wanted.astype(jnp.int32), axis=1) - 1
    picked = wanted[:, :, None] & (
        ranks[:, :, None] == jnp.arange(capacity, dtype=jnp.int32)[None, None, :]
    )
    send_places = jnp.sum(jnp.where(picked, places[:, :, None], 0), axis=1)
    outgoing = pool_kv[send_places.reshape(-1)].reshape(block_count, capacity, 2, page_len, width)
    arrived = lax.all_to_all(outgoing, "blk", split_axis=0, concat_axis=0, tiled=True)
    my_owners = lax.dynamic_index_in_dim(owners, block_index, 0, keepdims=False)
    order = jnp.arange(entries, dtype=jnp.int32)
    before = (my_owners[None, :] == my_owners[:, None]) & (order[None, :] < order[:, None])
    slots = my_owners * capacity + jnp.sum(before.astype(jnp.int32), axis=1)
    fetched = arrived.reshape(block_count * capacity, 2, page_len, width)[slots]
    cache_len = entries * page_len
    key_rows = jnp.concatenate([fetched[:, 0].reshape(cache_len, width), short_k], 0)
    value_rows = jnp.concatenate([fetched[:, 1].reshape(cache_len, width), short_v], 0)
    segment = short_seg[0]
    positions = jnp.arange(pack_rows, dtype=jnp.int32)
    key_seg = jnp.concatenate([jnp.arange(cache_len, dtype=jnp.int32) // (PPS * page_len), segment])
    key_pos = jnp.concatenate([jnp.full((cache_len,), -1, jnp.int32), positions])
    allowed = ((key_seg[None, :] == segment[:, None]) & (key_pos[None, :] <= positions[:, None]))[
        None
    ]
    query_heads = short_q.reshape(pack_rows, heads_dev, HD)
    key_heads = key_rows.reshape(cache_len + pack_rows, heads_dev, HD)
    value_heads = value_rows.reshape(cache_len + pack_rows, heads_dev, HD)
    scores = jnp.einsum(
        "qhd,khd->hqk", query_heads, key_heads, preferred_element_type=jnp.float32
    ) * HD ** (-0.5)
    scores = jnp.where(allowed, scores, very_negative)
    row_max = jnp.max(scores, axis=-1)
    weights = jnp.where(allowed, jnp.exp(scores - row_max[..., None]), 0.0)
    total = jnp.sum(weights, axis=-1)
    numer = jnp.einsum(
        "hqk,khd->hqd",
        weights.astype(jnp.bfloat16),
        value_heads,
        preferred_element_type=jnp.float32,
    )
    merged = numer / total[..., None]
    return merged.transpose(1, 0, 2).reshape(pack_rows, width).astype(jnp.bfloat16)


def per_device(
    long_q, long_k, long_v, short_q, short_k, short_v, short_seg, pool_kv, page_table, w_out
):
    block_count = lax.axis_size("blk")
    block_index = lax.axis_index("blk")
    long_attn = prompt_attention(long_q, block_index, long_k, long_v)
    short_attn = pack_attention(
        short_q, short_k, short_v, short_seg, pool_kv, page_table, block_index, block_count
    )
    long_rows = lax.all_to_all(long_attn, "req", 0, 1, tiled=True)
    short_rows = lax.all_to_all(short_attn, "req", 0, 1, tiled=True)
    long_out = jnp.dot(long_rows, w_out, preferred_element_type=jnp.float32).astype(jnp.bfloat16)
    short_out = jnp.dot(short_rows, w_out, preferred_element_type=jnp.float32).astype(jnp.bfloat16)
    return (long_out, short_out)


def solution(mesh):
    placed = (
        P("blk", "req"),
        P("blk", "req"),
        P("blk", "req"),
        P("blk", "req"),
        P("blk", "req"),
        P("blk", "req"),
        P("blk", None),
        P("blk", None, None, "req"),
        P(),
        P(),
    )
    return jax.shard_map(
        per_device,
        mesh=mesh,
        in_specs=placed,
        out_specs=(P(("blk", "req"), None), P(("blk", "req"), None)),
        check_vma=False,
    )
```

```python
import functools
import math

import jax
import jax.numpy as jnp
from jax import lax
from jax.experimental import pallas as pl
from jax.experimental.pallas import tpu as pltpu
from jax.sharding import PartitionSpec as P

HD = 128
PPS = 4


very_negative = -1e30


def flash_body(pos_ref, q_ref, a_ref, b_ref, o_ref, m_sc, l_sc, acc_sc, *, tq, tk, q_rows):
    q_tile = pl.program_id(0)
    k_tile = pl.program_id(1)
    first_query = pos_ref[0] * q_rows + q_tile * tq
    last_tile = (first_query + tq - 1) // tk

    @pl.when(k_tile == 0)
    def _():
        m_sc[...] = jnp.full(m_sc.shape, very_negative, jnp.float32)
        l_sc[...] = jnp.zeros(l_sc.shape, jnp.float32)
        acc_sc[...] = jnp.zeros(acc_sc.shape, jnp.float32)

    def fold(masked, k_ref, v_ref):
        scores = lax.dot_general(
            q_ref[...], k_ref[...], (((1,), (1,)), ((), ())),
            preferred_element_type=jnp.float32,
        ) * HD ** (-0.5)
        if masked:
            query_pos = first_query + lax.broadcasted_iota(jnp.int32, (tq, tk), 0)
            key_pos = k_tile * tk + lax.broadcasted_iota(jnp.int32, (tq, tk), 1)
            scores = jnp.where(key_pos <= query_pos, scores, very_negative)
        run_max = m_sc[...]
        new_max = jnp.maximum(run_max, jnp.max(scores, axis=1, keepdims=True))
        weights = jnp.exp(scores - new_max[:, :1])
        factor = jnp.exp(run_max - new_max)
        l_sc[...] = l_sc[...] * factor + jnp.sum(weights, axis=1, keepdims=True)
        m_sc[...] = new_max
        acc_sc[...] = acc_sc[...] * factor + jnp.dot(
            weights.astype(jnp.bfloat16), v_ref[...], preferred_element_type=jnp.float32
        )

    needs_mask = (k_tile + 1) * tk - 1 > first_query
    live = k_tile <= last_tile
    keys_first = pos_ref[1] == 0
    for masked in (False, True):
        mask_case = needs_mask if masked else jnp.logical_not(needs_mask)

        @pl.when(live & mask_case & keys_first)
        def _():
            fold(masked, a_ref, b_ref)

        @pl.when(live & mask_case & jnp.logical_not(keys_first))
        def _():
            fold(masked, b_ref, a_ref)

    @pl.when(k_tile == last_tile)
    def _():
        o_ref[...] = (acc_sc[...] / l_sc[...]).astype(o_ref.dtype)


def flash_head(queries, head, block_index, core, first_piece, second_piece):
    row_count = queries.shape[0]
    piece_rows = first_piece.shape[0]
    tq = min(row_count, 512)
    tk = min(row_count, 1024)

    def kv_map(q_tile, k_tile, pos_ref):
        last_tile = (pos_ref[0] * row_count + q_tile * tq + tq - 1) // tk
        return (jnp.minimum(k_tile, last_tile), 0)

    body = functools.partial(flash_body, tq=tq, tk=tk, q_rows=row_count)
    return pl.pallas_call(
        body,
        out_shape=jax.ShapeDtypeStruct((row_count, HD), jnp.bfloat16),
        grid_spec=pltpu.PrefetchScalarGridSpec(
            num_scalar_prefetch=1,
            grid=(row_count // tq, piece_rows // tk),
            in_specs=[
                pl.BlockSpec((tq, HD), lambda q_tile, k_tile, pos_ref: (q_tile, head)),
                pl.BlockSpec((tk, HD), kv_map),
                pl.BlockSpec((tk, HD), kv_map),
            ],
            out_specs=pl.BlockSpec((tq, HD), lambda q_tile, k_tile, pos_ref: (q_tile, 0)),
            scratch_shapes=[
                pltpu.VMEM((tq, HD), jnp.float32),
                pltpu.VMEM((tq, HD), jnp.float32),
                pltpu.VMEM((tq, HD), jnp.float32),
            ],
        ),
        compiler_params=pltpu.CompilerParams(dimension_semantics=("arbitrary", "arbitrary")),
    )(jnp.stack([block_index, core]).astype(jnp.int32), queries, first_piece, second_piece)


def prompt_attention(queries, block_index, core, long_k, long_v):
    heads_dev = queries.shape[1] // HD
    swap = [(0, 1), (1, 0)]
    outs = []
    for head in range(heads_dev):
        cols = slice(head * HD, (head + 1) * HD)
        key_head = long_k[:, cols]
        value_head = long_v[:, cols]
        first_core = core == 0
        partner = lax.ppermute(jnp.where(first_core, value_head, key_head), "core", swap)
        pair = jnp.where(
            first_core,
            jnp.concatenate([key_head, partner], 0),
            jnp.concatenate([partner, value_head], 0),
        )
        first_piece = lax.all_gather(pair, "chip", axis=0, tiled=True)
        second_piece = lax.ppermute(first_piece, "core", swap)
        outs.append(flash_head(queries, head, block_index, core, first_piece, second_piece))
    return jnp.concatenate(outs, 1)


def pack_attention(
    short_q, short_k, short_v, short_seg, pool_kv, page_table, block_index, block_count
):
    pack_rows, width = short_q.shape
    heads_dev = width // HD
    pool_pages = pool_kv.shape[0]
    page_len = pool_kv.shape[2]
    page_rows = page_table.reshape(block_count, -1)
    entries = page_rows.shape[1]
    capacity = entries // block_count
    owners = page_rows // pool_pages
    places = page_rows % pool_pages
    wanted = owners == block_index
    ranks = jnp.cumsum(wanted.astype(jnp.int32), axis=1) - 1
    picked = wanted[:, :, None] & (
        ranks[:, :, None] == jnp.arange(capacity, dtype=jnp.int32)[None, None, :]
    )
    send_places = jnp.sum(jnp.where(picked, places[:, :, None], 0), axis=1)
    outgoing = pool_kv[send_places.reshape(-1)].reshape(block_count, capacity, 2, page_len, width)
    arrived = lax.all_to_all(outgoing, ("chip", "core"), split_axis=0, concat_axis=0, tiled=True)
    my_owners = lax.dynamic_index_in_dim(owners, block_index, 0, keepdims=False)
    order = jnp.arange(entries, dtype=jnp.int32)
    before = (my_owners[None, :] == my_owners[:, None]) & (order[None, :] < order[:, None])
    slots = my_owners * capacity + jnp.sum(before.astype(jnp.int32), axis=1)
    fetched = arrived.reshape(block_count * capacity, 2, page_len, width)[slots]
    cache_len = entries * page_len
    key_rows = jnp.concatenate([fetched[:, 0].reshape(cache_len, width), short_k], 0)
    value_rows = jnp.concatenate([fetched[:, 1].reshape(cache_len, width), short_v], 0)
    segment = short_seg[0]
    positions = jnp.arange(pack_rows, dtype=jnp.int32)
    key_seg = jnp.concatenate([jnp.arange(cache_len, dtype=jnp.int32) // (PPS * page_len), segment])
    key_pos = jnp.concatenate([jnp.full((cache_len,), -1, jnp.int32), positions])
    allowed = ((key_seg[None, :] == segment[:, None]) & (key_pos[None, :] <= positions[:, None]))[
        None
    ]
    query_heads = short_q.reshape(pack_rows, heads_dev, HD)
    key_heads = key_rows.reshape(cache_len + pack_rows, heads_dev, HD)
    value_heads = value_rows.reshape(cache_len + pack_rows, heads_dev, HD)
    scores = jnp.einsum(
        "qhd,khd->hqk", query_heads, key_heads, preferred_element_type=jnp.float32
    ) * HD ** (-0.5)
    scores = jnp.where(allowed, scores, very_negative)
    row_max = jnp.max(scores, axis=-1)
    weights = jnp.where(allowed, jnp.exp(scores - row_max[..., None]), 0.0)
    total = jnp.sum(weights, axis=-1)
    numer = jnp.einsum(
        "hqk,khd->hqd",
        weights.astype(jnp.bfloat16),
        value_heads,
        preferred_element_type=jnp.float32,
    )
    merged = numer / total[..., None]
    return merged.transpose(1, 0, 2).reshape(pack_rows, width).astype(jnp.bfloat16)


def per_device(
    long_q, long_k, long_v, short_q, short_k, short_v, short_seg, pool_kv, page_table, w_out
):
    block_count = lax.axis_size("chip") * lax.axis_size("core")
    core = lax.axis_index("core")
    block_index = lax.axis_index("chip") * lax.axis_size("core") + core
    long_attn = prompt_attention(long_q, block_index, core, long_k, long_v)
    short_attn = pack_attention(
        short_q, short_k, short_v, short_seg, pool_kv, page_table, block_index, block_count
    )
    long_rows = lax.all_to_all(long_attn, "req", 0, 1, tiled=True)
    short_rows = lax.all_to_all(short_attn, "req", 0, 1, tiled=True)
    long_out = jnp.dot(long_rows, w_out, preferred_element_type=jnp.float32).astype(jnp.bfloat16)
    short_out = jnp.dot(short_rows, w_out, preferred_element_type=jnp.float32).astype(jnp.bfloat16)
    return (long_out, short_out)


def solution(mesh):
    chips = mesh.shape["blk"] // 2
    mesh = jax.sharding.Mesh(
        mesh.devices.reshape(chips, 2, mesh.shape["req"]), ("chip", "core", "req")
    )
    blk = ("chip", "core")
    placed = (
        P(blk, "req"),
        P(blk, "req"),
        P(blk, "req"),
        P(blk, "req"),
        P(blk, "req"),
        P(blk, "req"),
        P(blk, None),
        P(blk, None, None, "req"),
        P(),
        P(),
    )
    return jax.shard_map(
        per_device,
        mesh=mesh,
        in_specs=placed,
        out_specs=(P(blk + ("req",), None), P(blk + ("req",), None)),
        check_vma=False,
    )
```

```python
import functools
import math

import jax
import jax.numpy as jnp
from jax import lax
from jax.experimental import pallas as pl
from jax.experimental.pallas import tpu as pltpu
from jax.sharding import PartitionSpec as P

HD = 128
PPS = 4


very_negative = -1e30


def flash_body(blk_ref, q_ref, k_ref, v_ref, o_ref, m_sc, l_sc, acc_sc, *, heads, tq, tk, q_rows):
    q_tile = pl.program_id(0)
    k_tile = pl.program_id(1)
    first_query = blk_ref[0] * q_rows + q_tile * tq
    last_tile = (first_query + tq - 1) // tk

    @pl.when(k_tile == 0)
    def _():
        m_sc[...] = jnp.full(m_sc.shape, very_negative, jnp.float32)
        l_sc[...] = jnp.zeros(l_sc.shape, jnp.float32)
        acc_sc[...] = jnp.zeros(acc_sc.shape, jnp.float32)

    def fold(masked):
        for h in range(heads):
            cols = slice(h * HD, (h + 1) * HD)
            scores = lax.dot_general(
                q_ref[:, cols], k_ref[:, cols], (((1,), (1,)), ((), ())),
                preferred_element_type=jnp.float32,
            ) * HD ** (-0.5)
            if masked:
                query_pos = first_query + lax.broadcasted_iota(jnp.int32, (tq, tk), 0)
                key_pos = k_tile * tk + lax.broadcasted_iota(jnp.int32, (tq, tk), 1)
                scores = jnp.where(key_pos <= query_pos, scores, very_negative)
            run_max = m_sc[h]
            new_max = jnp.maximum(run_max, jnp.max(scores, axis=1, keepdims=True))
            weights = jnp.exp(scores - new_max[:, :1])
            factor = jnp.exp(run_max - new_max)
            l_sc[h] = l_sc[h] * factor + jnp.sum(weights, axis=1, keepdims=True)
            m_sc[h] = new_max
            acc_sc[h] = acc_sc[h] * factor + jnp.dot(
                weights.astype(jnp.bfloat16), v_ref[:, cols], preferred_element_type=jnp.float32
            )

    needs_mask = (k_tile + 1) * tk - 1 > first_query

    @pl.when((k_tile <= last_tile) & jnp.logical_not(needs_mask))
    def _():
        fold(False)

    @pl.when((k_tile <= last_tile) & needs_mask)
    def _():
        fold(True)

    @pl.when(k_tile == last_tile)
    def _():
        for h in range(heads):
            o_ref[:, h * HD:(h + 1) * HD] = (acc_sc[h] / l_sc[h]).astype(o_ref.dtype)


def prompt_attention(queries, block_index, long_k, long_v):
    row_count, width = queries.shape
    heads_dev = width // HD
    block_count = lax.axis_size("blk")
    own = jnp.concatenate([long_k, long_v], 1)
    pieces = [own]
    for shift in range(1, block_count):
        pairs = [(src, src + shift) for src in range(block_count - shift)]
        pieces.append(lax.ppermute(own, "blk", pairs))
    stacked = jnp.stack(pieces)
    piece_rows = block_count * row_count
    tq = min(row_count, 512)
    tk = min(row_count, 1024)

    def kv_map(column):
        def index(q_tile, k_tile, blk_ref):
            last_tile = (blk_ref[0] * row_count + q_tile * tq + tq - 1) // tk
            return (blk_ref[0] - jnp.minimum(k_tile, last_tile), 0, column)

        return index

    body = functools.partial(flash_body, heads=heads_dev, tq=tq, tk=tk, q_rows=row_count)
    return pl.pallas_call(
        body,
        out_shape=jax.ShapeDtypeStruct((row_count, width), jnp.bfloat16),
        grid_spec=pltpu.PrefetchScalarGridSpec(
            num_scalar_prefetch=1,
            grid=(row_count // tq, piece_rows // tk),
            in_specs=[
                pl.BlockSpec((tq, width), lambda q_tile, k_tile, blk_ref: (q_tile, 0)),
                pl.BlockSpec((None, tk, width), kv_map(0)),
                pl.BlockSpec((None, tk, width), kv_map(1)),
            ],
            out_specs=pl.BlockSpec((tq, width), lambda q_tile, k_tile, blk_ref: (q_tile, 0)),
            scratch_shapes=[
                pltpu.VMEM((heads_dev, tq, HD), jnp.float32),
                pltpu.VMEM((heads_dev, tq, HD), jnp.float32),
                pltpu.VMEM((heads_dev, tq, HD), jnp.float32),
            ],
        ),
        compiler_params=pltpu.CompilerParams(dimension_semantics=("arbitrary", "arbitrary")),
    )(jnp.reshape(block_index, (1,)).astype(jnp.int32), queries, stacked, stacked)


def pack_attention(
    short_q, short_k, short_v, short_seg, pool_kv, page_table, block_index, block_count
):
    pack_rows, width = short_q.shape
    heads_dev = width // HD
    pool_pages = pool_kv.shape[0]
    page_len = pool_kv.shape[2]
    page_rows = page_table.reshape(block_count, -1)
    entries = page_rows.shape[1]
    capacity = entries // block_count
    owners = page_rows // pool_pages
    places = page_rows % pool_pages
    wanted = owners == block_index
    ranks = jnp.cumsum(wanted.astype(jnp.int32), axis=1) - 1
    picked = wanted[:, :, None] & (
        ranks[:, :, None] == jnp.arange(capacity, dtype=jnp.int32)[None, None, :]
    )
    send_places = jnp.sum(jnp.where(picked, places[:, :, None], 0), axis=1)
    outgoing = pool_kv[send_places.reshape(-1)].reshape(block_count, capacity, 2, page_len, width)
    arrived = lax.all_to_all(outgoing, "blk", split_axis=0, concat_axis=0, tiled=True)
    my_owners = lax.dynamic_index_in_dim(owners, block_index, 0, keepdims=False)
    order = jnp.arange(entries, dtype=jnp.int32)
    before = (my_owners[None, :] == my_owners[:, None]) & (order[None, :] < order[:, None])
    slots = my_owners * capacity + jnp.sum(before.astype(jnp.int32), axis=1)
    fetched = arrived.reshape(block_count * capacity, 2, page_len, width)[slots]
    cache_len = entries * page_len
    key_rows = jnp.concatenate([fetched[:, 0].reshape(cache_len, width), short_k], 0)
    value_rows = jnp.concatenate([fetched[:, 1].reshape(cache_len, width), short_v], 0)
    segment = short_seg[0]
    positions = jnp.arange(pack_rows, dtype=jnp.int32)
    key_seg = jnp.concatenate([jnp.arange(cache_len, dtype=jnp.int32) // (PPS * page_len), segment])
    key_pos = jnp.concatenate([jnp.full((cache_len,), -1, jnp.int32), positions])
    allowed = ((key_seg[None, :] == segment[:, None]) & (key_pos[None, :] <= positions[:, None]))[
        None
    ]
    query_heads = short_q.reshape(pack_rows, heads_dev, HD)
    key_heads = key_rows.reshape(cache_len + pack_rows, heads_dev, HD)
    value_heads = value_rows.reshape(cache_len + pack_rows, heads_dev, HD)
    scores = jnp.einsum(
        "qhd,khd->hqk", query_heads, key_heads, preferred_element_type=jnp.float32
    ) * HD ** (-0.5)
    scores = jnp.where(allowed, scores, very_negative)
    row_max = jnp.max(scores, axis=-1)
    weights = jnp.where(allowed, jnp.exp(scores - row_max[..., None]), 0.0)
    total = jnp.sum(weights, axis=-1)
    numer = jnp.einsum(
        "hqk,khd->hqd",
        weights.astype(jnp.bfloat16),
        value_heads,
        preferred_element_type=jnp.float32,
    )
    merged = numer / total[..., None]
    return merged.transpose(1, 0, 2).reshape(pack_rows, width).astype(jnp.bfloat16)


def per_device(
    long_q, long_k, long_v, short_q, short_k, short_v, short_seg, pool_kv, page_table, w_out
):
    block_count = lax.axis_size("blk")
    block_index = lax.axis_index("blk")
    long_attn = prompt_attention(long_q, block_index, long_k, long_v)
    short_attn = pack_attention(
        short_q, short_k, short_v, short_seg, pool_kv, page_table, block_index, block_count
    )
    long_rows = lax.all_to_all(long_attn, "req", 0, 1, tiled=True)
    short_rows = lax.all_to_all(short_attn, "req", 0, 1, tiled=True)
    long_out = jnp.dot(long_rows, w_out, preferred_element_type=jnp.float32).astype(jnp.bfloat16)
    short_out = jnp.dot(short_rows, w_out, preferred_element_type=jnp.float32).astype(jnp.bfloat16)
    return (long_out, short_out)


def solution(mesh):
    placed = (
        P("blk", "req"),
        P("blk", "req"),
        P("blk", "req"),
        P("blk", "req"),
        P("blk", "req"),
        P("blk", "req"),
        P("blk", None),
        P("blk", None, None, "req"),
        P(),
        P(),
    )
    return jax.shard_map(
        per_device,
        mesh=mesh,
        in_specs=placed,
        out_specs=(P(("blk", "req"), None), P(("blk", "req"), None)),
        check_vma=False,
    )
```

```python
import functools
import math

import jax
import jax.numpy as jnp
from jax import lax
from jax.experimental import pallas as pl
from jax.experimental.pallas import tpu as pltpu
from jax.sharding import PartitionSpec as P

HD = 128
PPS = 4


very_negative = -1e30


def flash_body(blk_ref, q_ref, k_ref, v_ref, o_ref, m_sc, l_sc, acc_sc, *, heads, tq, tk, q_rows):
    q_tile = pl.program_id(0)
    k_tile = pl.program_id(1)
    first_query = blk_ref[0] * q_rows + q_tile * tq
    last_tile = (first_query + tq - 1) // tk

    @pl.when(k_tile == 0)
    def _():
        m_sc[...] = jnp.full(m_sc.shape, very_negative, jnp.float32)
        l_sc[...] = jnp.zeros(l_sc.shape, jnp.float32)
        acc_sc[...] = jnp.zeros(acc_sc.shape, jnp.float32)

    def fold(masked):
        for h in range(heads):
            cols = slice(h * HD, (h + 1) * HD)
            scores = lax.dot_general(
                q_ref[:, cols], k_ref[:, cols], (((1,), (1,)), ((), ())),
                preferred_element_type=jnp.float32,
            ) * HD ** (-0.5)
            if masked:
                query_pos = first_query + lax.broadcasted_iota(jnp.int32, (tq, tk), 0)
                key_pos = k_tile * tk + lax.broadcasted_iota(jnp.int32, (tq, tk), 1)
                scores = jnp.where(key_pos <= query_pos, scores, very_negative)
            run_max = m_sc[h]
            new_max = jnp.maximum(run_max, jnp.max(scores, axis=1, keepdims=True))
            weights = jnp.exp(scores - new_max[:, :1])
            factor = jnp.exp(run_max - new_max)
            l_sc[h] = l_sc[h] * factor + jnp.sum(weights, axis=1, keepdims=True)
            m_sc[h] = new_max
            acc_sc[h] = acc_sc[h] * factor + jnp.dot(
                weights.astype(jnp.bfloat16), v_ref[:, cols], preferred_element_type=jnp.float32
            )

    needs_mask = (k_tile + 1) * tk - 1 > first_query

    @pl.when((k_tile <= last_tile) & jnp.logical_not(needs_mask))
    def _():
        fold(False)

    @pl.when((k_tile <= last_tile) & needs_mask)
    def _():
        fold(True)

    @pl.when(k_tile == last_tile)
    def _():
        for h in range(heads):
            o_ref[:, h * HD:(h + 1) * HD] = (acc_sc[h] / l_sc[h]).astype(o_ref.dtype)


def prompt_attention(queries, block_index, long_k, long_v, early=None):
    row_count, width = queries.shape
    heads_dev = width // HD
    kv_piece = lax.all_gather(jnp.concatenate([long_k, long_v], 1), "blk", axis=0, tiled=True)
    if early is not None:
        kv_piece, early = lax.optimization_barrier((kv_piece, early))
    piece_rows = kv_piece.shape[0]
    tq = min(row_count, 512)
    tk = min(row_count, 1024)

    def kv_map(column):
        def index(q_tile, k_tile, blk_ref):
            last_tile = (blk_ref[0] * row_count + q_tile * tq + tq - 1) // tk
            return (jnp.minimum(k_tile, last_tile), column)

        return index

    body = functools.partial(flash_body, heads=heads_dev, tq=tq, tk=tk, q_rows=row_count)
    return pl.pallas_call(
        body,
        out_shape=jax.ShapeDtypeStruct((row_count, width), jnp.bfloat16),
        grid_spec=pltpu.PrefetchScalarGridSpec(
            num_scalar_prefetch=1,
            grid=(row_count // tq, piece_rows // tk),
            in_specs=[
                pl.BlockSpec((tq, width), lambda q_tile, k_tile, blk_ref: (q_tile, 0)),
                pl.BlockSpec((tk, width), kv_map(0)),
                pl.BlockSpec((tk, width), kv_map(1)),
            ],
            out_specs=pl.BlockSpec((tq, width), lambda q_tile, k_tile, blk_ref: (q_tile, 0)),
            scratch_shapes=[
                pltpu.VMEM((heads_dev, tq, HD), jnp.float32),
                pltpu.VMEM((heads_dev, tq, HD), jnp.float32),
                pltpu.VMEM((heads_dev, tq, HD), jnp.float32),
            ],
        ),
        compiler_params=pltpu.CompilerParams(dimension_semantics=("arbitrary", "arbitrary")),
    )(jnp.reshape(block_index, (1,)).astype(jnp.int32), queries, kv_piece, kv_piece), early


def pack_attention(
    short_q, short_k, short_v, short_seg, pool_kv, page_table, block_index, block_count
):
    pack_rows, width = short_q.shape
    heads_dev = width // HD
    pool_pages = pool_kv.shape[0]
    page_len = pool_kv.shape[2]
    page_rows = page_table.reshape(block_count, -1)
    entries = page_rows.shape[1]
    capacity = entries // block_count
    owners = page_rows // pool_pages
    places = page_rows % pool_pages
    wanted = owners == block_index
    ranks = jnp.cumsum(wanted.astype(jnp.int32), axis=1) - 1
    picked = wanted[:, :, None] & (
        ranks[:, :, None] == jnp.arange(capacity, dtype=jnp.int32)[None, None, :]
    )
    send_places = jnp.sum(jnp.where(picked, places[:, :, None], 0), axis=1)
    outgoing = pool_kv[send_places.reshape(-1)].reshape(block_count, capacity, 2, page_len, width)
    arrived = lax.all_to_all(outgoing, "blk", split_axis=0, concat_axis=0, tiled=True)
    my_owners = lax.dynamic_index_in_dim(owners, block_index, 0, keepdims=False)
    order = jnp.arange(entries, dtype=jnp.int32)
    before = (my_owners[None, :] == my_owners[:, None]) & (order[None, :] < order[:, None])
    slots = my_owners * capacity + jnp.sum(before.astype(jnp.int32), axis=1)
    fetched = arrived.reshape(block_count * capacity, 2, page_len, width)[slots]
    cache_len = entries * page_len
    key_rows = jnp.concatenate([fetched[:, 0].reshape(cache_len, width), short_k], 0)
    value_rows = jnp.concatenate([fetched[:, 1].reshape(cache_len, width), short_v], 0)
    segment = short_seg[0]
    positions = jnp.arange(pack_rows, dtype=jnp.int32)
    key_seg = jnp.concatenate([jnp.arange(cache_len, dtype=jnp.int32) // (PPS * page_len), segment])
    key_pos = jnp.concatenate([jnp.full((cache_len,), -1, jnp.int32), positions])
    allowed = ((key_seg[None, :] == segment[:, None]) & (key_pos[None, :] <= positions[:, None]))[
        None
    ]
    query_heads = short_q.reshape(pack_rows, heads_dev, HD)
    key_heads = key_rows.reshape(cache_len + pack_rows, heads_dev, HD)
    value_heads = value_rows.reshape(cache_len + pack_rows, heads_dev, HD)
    scores = jnp.einsum(
        "qhd,khd->hqk", query_heads, key_heads, preferred_element_type=jnp.float32
    ) * HD ** (-0.5)
    scores = jnp.where(allowed, scores, very_negative)
    row_max = jnp.max(scores, axis=-1)
    weights = jnp.where(allowed, jnp.exp(scores - row_max[..., None]), 0.0)
    total = jnp.sum(weights, axis=-1)
    numer = jnp.einsum(
        "hqk,khd->hqd",
        weights.astype(jnp.bfloat16),
        value_heads,
        preferred_element_type=jnp.float32,
    )
    merged = numer / total[..., None]
    return merged.transpose(1, 0, 2).reshape(pack_rows, width).astype(jnp.bfloat16)


def per_device(
    long_q, long_k, long_v, short_q, short_k, short_v, short_seg, pool_kv, page_table, w_out
):
    block_count = lax.axis_size("blk")
    block_index = lax.axis_index("blk")
    short_attn = pack_attention(
        short_q, short_k, short_v, short_seg, pool_kv, page_table, block_index, block_count
    )
    short_rows = lax.all_to_all(short_attn, "req", 0, 1, tiled=True)
    short_out = jnp.dot(short_rows, w_out, preferred_element_type=jnp.float32).astype(jnp.bfloat16)
    long_attn, short_out = prompt_attention(long_q, block_index, long_k, long_v, short_out)
    long_rows = lax.all_to_all(long_attn, "req", 0, 1, tiled=True)
    long_out = jnp.dot(long_rows, w_out, preferred_element_type=jnp.float32).astype(jnp.bfloat16)
    return (long_out, short_out)


def solution(mesh):
    placed = (
        P("blk", "req"),
        P("blk", "req"),
        P("blk", "req"),
        P("blk", "req"),
        P("blk", "req"),
        P("blk", "req"),
        P("blk", None),
        P("blk", None, None, "req"),
        P(),
        P(),
    )
    return jax.shard_map(
        per_device,
        mesh=mesh,
        in_specs=placed,
        out_specs=(P(("blk", "req"), None), P(("blk", "req"), None)),
        check_vma=False,
    )
```

```python
import functools
import math

import jax
import jax.numpy as jnp
from jax import lax
from jax.experimental import pallas as pl
from jax.experimental.pallas import tpu as pltpu
from jax.sharding import PartitionSpec as P

HD = 128
PPS = 4


very_negative = -1e30


def flash_body(blk_ref, q_ref, k_ref, v_ref, o_ref, m_sc, l_sc, acc_sc, *, heads, tq, tk, q_rows):
    q_tile = pl.program_id(0)
    k_tile = pl.program_id(1)
    first_query = blk_ref[q_tile] * q_rows + q_tile * tq
    last_tile = (first_query + tq - 1) // tk

    @pl.when(k_tile == 0)
    def _():
        m_sc[...] = jnp.full(m_sc.shape, very_negative, jnp.float32)
        l_sc[...] = jnp.zeros(l_sc.shape, jnp.float32)
        acc_sc[...] = jnp.zeros(acc_sc.shape, jnp.float32)

    def fold(masked):
        for h in range(heads):
            cols = slice(h * HD, (h + 1) * HD)
            scores = lax.dot_general(
                q_ref[:, cols], k_ref[:, cols], (((1,), (1,)), ((), ())),
                preferred_element_type=jnp.float32,
            ) * HD ** (-0.5)
            if masked:
                query_pos = first_query + lax.broadcasted_iota(jnp.int32, (tq, tk), 0)
                key_pos = k_tile * tk + lax.broadcasted_iota(jnp.int32, (tq, tk), 1)
                scores = jnp.where(key_pos <= query_pos, scores, very_negative)
            run_max = m_sc[h]
            new_max = jnp.maximum(run_max, jnp.max(scores, axis=1, keepdims=True))
            weights = jnp.exp(scores - new_max[:, :1])
            factor = jnp.exp(run_max - new_max)
            l_sc[h] = l_sc[h] * factor + jnp.sum(weights, axis=1, keepdims=True)
            m_sc[h] = new_max
            acc_sc[h] = acc_sc[h] * factor + jnp.dot(
                weights.astype(jnp.bfloat16), v_ref[:, cols], preferred_element_type=jnp.float32
            )

    needs_mask = (k_tile + 1) * tk - 1 > first_query

    @pl.when((k_tile <= last_tile) & jnp.logical_not(needs_mask))
    def _():
        fold(False)

    @pl.when((k_tile <= last_tile) & needs_mask)
    def _():
        fold(True)

    @pl.when(k_tile == last_tile)
    def _():
        for h in range(heads):
            o_ref[:, h * HD:(h + 1) * HD] = (acc_sc[h] / l_sc[h]).astype(o_ref.dtype)


def prompt_attention(queries, block_index, long_k, long_v, early=None):
    row_count, width = queries.shape
    heads_dev = width // HD
    kv_piece = lax.all_gather(jnp.concatenate([long_k, long_v], 1), "blk", axis=0, tiled=True)
    if early is not None:
        kv_piece, early = lax.optimization_barrier((kv_piece, early))
    piece_rows = kv_piece.shape[0]
    block_count = lax.axis_size("blk")
    tq = row_count // 2
    mirror = [(src, block_count - 1 - src) for src in range(block_count)]
    partner_half = lax.ppermute(queries[tq:], "blk", mirror)
    tile_blocks = jnp.stack([block_index, block_count - 1 - block_index]).astype(jnp.int32)
    tk = min(row_count, 1024)

    def kv_map(column):
        def index(q_tile, k_tile, blk_ref):
            last_tile = (blk_ref[q_tile] * row_count + q_tile * tq + tq - 1) // tk
            return (jnp.minimum(k_tile, last_tile), column)

        return index

    body = functools.partial(flash_body, heads=heads_dev, tq=tq, tk=tk, q_rows=row_count)
    result = pl.pallas_call(
        body,
        out_shape=jax.ShapeDtypeStruct((row_count, width), jnp.bfloat16),
        grid_spec=pltpu.PrefetchScalarGridSpec(
            num_scalar_prefetch=1,
            grid=(row_count // tq, piece_rows // tk),
            in_specs=[
                pl.BlockSpec((tq, width), lambda q_tile, k_tile, blk_ref: (q_tile, 0)),
                pl.BlockSpec((tk, width), kv_map(0)),
                pl.BlockSpec((tk, width), kv_map(1)),
            ],
            out_specs=pl.BlockSpec((tq, width), lambda q_tile, k_tile, blk_ref: (q_tile, 0)),
            scratch_shapes=[
                pltpu.VMEM((heads_dev, tq, HD), jnp.float32),
                pltpu.VMEM((heads_dev, tq, HD), jnp.float32),
                pltpu.VMEM((heads_dev, tq, HD), jnp.float32),
            ],
        ),
        compiler_params=pltpu.CompilerParams(dimension_semantics=("arbitrary", "arbitrary")),
    )(tile_blocks, jnp.concatenate([queries[:tq], partner_half], 0), kv_piece, kv_piece)
    merged = jnp.concatenate([result[:tq], lax.ppermute(result[tq:], "blk", mirror)], 0)
    return merged, early


def pack_attention(
    short_q, short_k, short_v, short_seg, pool_kv, page_table, block_index, block_count
):
    pack_rows, width = short_q.shape
    heads_dev = width // HD
    pool_pages = pool_kv.shape[0]
    page_len = pool_kv.shape[2]
    page_rows = page_table.reshape(block_count, -1)
    entries = page_rows.shape[1]
    capacity = entries // block_count
    owners = page_rows // pool_pages
    places = page_rows % pool_pages
    wanted = owners == block_index
    ranks = jnp.cumsum(wanted.astype(jnp.int32), axis=1) - 1
    picked = wanted[:, :, None] & (
        ranks[:, :, None] == jnp.arange(capacity, dtype=jnp.int32)[None, None, :]
    )
    send_places = jnp.sum(jnp.where(picked, places[:, :, None], 0), axis=1)
    outgoing = pool_kv[send_places.reshape(-1)].reshape(block_count, capacity, 2, page_len, width)
    arrived = lax.all_to_all(outgoing, "blk", split_axis=0, concat_axis=0, tiled=True)
    my_owners = lax.dynamic_index_in_dim(owners, block_index, 0, keepdims=False)
    order = jnp.arange(entries, dtype=jnp.int32)
    before = (my_owners[None, :] == my_owners[:, None]) & (order[None, :] < order[:, None])
    slots = my_owners * capacity + jnp.sum(before.astype(jnp.int32), axis=1)
    fetched = arrived.reshape(block_count * capacity, 2, page_len, width)[slots]
    cache_len = entries * page_len
    key_rows = jnp.concatenate([fetched[:, 0].reshape(cache_len, width), short_k], 0)
    value_rows = jnp.concatenate([fetched[:, 1].reshape(cache_len, width), short_v], 0)
    segment = short_seg[0]
    positions = jnp.arange(pack_rows, dtype=jnp.int32)
    key_seg = jnp.concatenate([jnp.arange(cache_len, dtype=jnp.int32) // (PPS * page_len), segment])
    key_pos = jnp.concatenate([jnp.full((cache_len,), -1, jnp.int32), positions])
    allowed = ((key_seg[None, :] == segment[:, None]) & (key_pos[None, :] <= positions[:, None]))[
        None
    ]
    query_heads = short_q.reshape(pack_rows, heads_dev, HD)
    key_heads = key_rows.reshape(cache_len + pack_rows, heads_dev, HD)
    value_heads = value_rows.reshape(cache_len + pack_rows, heads_dev, HD)
    scores = jnp.einsum(
        "qhd,khd->hqk", query_heads, key_heads, preferred_element_type=jnp.float32
    ) * HD ** (-0.5)
    scores = jnp.where(allowed, scores, very_negative)
    row_max = jnp.max(scores, axis=-1)
    weights = jnp.where(allowed, jnp.exp(scores - row_max[..., None]), 0.0)
    total = jnp.sum(weights, axis=-1)
    numer = jnp.einsum(
        "hqk,khd->hqd",
        weights.astype(jnp.bfloat16),
        value_heads,
        preferred_element_type=jnp.float32,
    )
    merged = numer / total[..., None]
    return merged.transpose(1, 0, 2).reshape(pack_rows, width).astype(jnp.bfloat16)


def per_device(
    long_q, long_k, long_v, short_q, short_k, short_v, short_seg, pool_kv, page_table, w_out
):
    block_count = lax.axis_size("blk")
    block_index = lax.axis_index("blk")
    short_attn = pack_attention(
        short_q, short_k, short_v, short_seg, pool_kv, page_table, block_index, block_count
    )
    short_rows = lax.all_to_all(short_attn, "req", 0, 1, tiled=True)
    short_out = jnp.dot(short_rows, w_out, preferred_element_type=jnp.float32).astype(jnp.bfloat16)
    long_attn, short_out = prompt_attention(long_q, block_index, long_k, long_v, short_out)
    long_rows = lax.all_to_all(long_attn, "req", 0, 1, tiled=True)
    long_out = jnp.dot(long_rows, w_out, preferred_element_type=jnp.float32).astype(jnp.bfloat16)
    return (long_out, short_out)


def solution(mesh):
    placed = (
        P("blk", "req"),
        P("blk", "req"),
        P("blk", "req"),
        P("blk", "req"),
        P("blk", "req"),
        P("blk", "req"),
        P("blk", None),
        P("blk", None, None, "req"),
        P(),
        P(),
    )
    return jax.shard_map(
        per_device,
        mesh=mesh,
        in_specs=placed,
        out_specs=(P(("blk", "req"), None), P(("blk", "req"), None)),
        check_vma=False,
    )
```

```python
import functools
import math

import jax
import jax.numpy as jnp
from jax import lax
from jax.experimental import pallas as pl
from jax.experimental.pallas import tpu as pltpu
from jax.sharding import PartitionSpec as P

HD = 128
PPS = 4


very_negative = -1e30


def flash_body(pos_ref, q_ref, k_ref, v_ref, o_ref, m_sc, l_sc, acc_sc, *, tq, tk):
    q_tile = pl.program_id(0)
    k_tile = pl.program_id(1)
    first_query = pos_ref[q_tile]
    last_tile = (first_query + tq - 1) // tk

    @pl.when(k_tile == 0)
    def _():
        m_sc[...] = jnp.full(m_sc.shape, very_negative, jnp.float32)
        l_sc[...] = jnp.zeros(l_sc.shape, jnp.float32)
        acc_sc[...] = jnp.zeros(acc_sc.shape, jnp.float32)

    def fold(masked):
        scores = lax.dot_general(
            q_ref[...], k_ref[...], (((1,), (1,)), ((), ())),
            preferred_element_type=jnp.float32,
        ) * HD ** (-0.5)
        if masked:
            query_pos = first_query + lax.broadcasted_iota(jnp.int32, (tq, tk), 0)
            key_pos = k_tile * tk + lax.broadcasted_iota(jnp.int32, (tq, tk), 1)
            scores = jnp.where(key_pos <= query_pos, scores, very_negative)
        run_max = m_sc[...]
        new_max = jnp.maximum(run_max, jnp.max(scores, axis=1, keepdims=True))
        weights = jnp.exp(scores - new_max[:, :1])
        factor = jnp.exp(run_max - new_max)
        l_sc[...] = l_sc[...] * factor + jnp.sum(weights, axis=1, keepdims=True)
        m_sc[...] = new_max
        acc_sc[...] = acc_sc[...] * factor + jnp.dot(
            weights.astype(jnp.bfloat16), v_ref[...], preferred_element_type=jnp.float32
        )

    needs_mask = (k_tile + 1) * tk - 1 > first_query

    @pl.when((k_tile <= last_tile) & jnp.logical_not(needs_mask))
    def _():
        fold(False)

    @pl.when((k_tile <= last_tile) & needs_mask)
    def _():
        fold(True)

    @pl.when(k_tile == last_tile)
    def _():
        o_ref[...] = (acc_sc[...] / l_sc[...]).astype(o_ref.dtype)


def flash_call(tile_first, queries, kv_piece, tq, tk):
    row_count = queries.shape[0]

    def kv_map(column):
        def index(q_tile, k_tile, pos_ref):
            last_tile = (pos_ref[q_tile] + tq - 1) // tk
            return (jnp.minimum(k_tile, last_tile), column)

        return index

    body = functools.partial(flash_body, tq=tq, tk=tk)
    return pl.pallas_call(
        body,
        out_shape=jax.ShapeDtypeStruct((row_count, HD), jnp.bfloat16),
        grid_spec=pltpu.PrefetchScalarGridSpec(
            num_scalar_prefetch=1,
            grid=(row_count // tq, kv_piece.shape[0] // tk),
            in_specs=[
                pl.BlockSpec((tq, HD), lambda q_tile, k_tile, pos_ref: (q_tile, 0)),
                pl.BlockSpec((tk, HD), kv_map(0)),
                pl.BlockSpec((tk, HD), kv_map(1)),
            ],
            out_specs=pl.BlockSpec((tq, HD), lambda q_tile, k_tile, pos_ref: (q_tile, 0)),
            scratch_shapes=[
                pltpu.VMEM((tq, HD), jnp.float32),
                pltpu.VMEM((tq, HD), jnp.float32),
                pltpu.VMEM((tq, HD), jnp.float32),
            ],
        ),
        compiler_params=pltpu.CompilerParams(dimension_semantics=("arbitrary", "arbitrary")),
    )(tile_first, queries, kv_piece, kv_piece)


def prompt_attention(long_q, long_k, long_v, chip, core, early):
    row_count, width = long_q.shape
    chip_count = lax.axis_size("chip")
    swap = [(0, 1), (1, 0)]
    first_core = core == 0
    packed = jnp.concatenate([long_q, long_k, long_v], 1).reshape(row_count, 3, 2, HD)
    mine = jnp.where(first_core, packed[:, :, 0], packed[:, :, 1]).reshape(row_count, 3 * HD)
    given = jnp.where(first_core, packed[:, :, 1], packed[:, :, 0]).reshape(row_count, 3 * HD)
    partner = lax.ppermute(given, "core", swap)
    pair = jnp.where(
        first_core,
        jnp.concatenate([mine, partner], 0),
        jnp.concatenate([partner, mine], 0),
    )
    kv_piece = lax.all_gather(pair[:, HD:], "chip", axis=0, tiled=True)
    kv_piece, early = lax.optimization_barrier((kv_piece, early))
    chip_rows = 2 * row_count
    tq = chip_rows // 4
    tk = min(row_count, 1024)
    mirror = [(src, chip_count - 1 - src) for src in range(chip_count)]
    queries = pair[:, :HD]
    lent = lax.ppermute(queries[tq:3 * tq], "chip", mirror)
    other = chip_count - 1 - chip
    tile_first = jnp.stack(
        [chip * chip_rows, chip * chip_rows + 3 * tq, other * chip_rows + tq, other * chip_rows + 2 * tq]
    ).astype(jnp.int32)
    result = flash_call(
        tile_first, jnp.concatenate([queries[:tq], queries[3 * tq:], lent], 0), kv_piece, tq, tk
    )
    back = lax.ppermute(result[2 * tq:], "chip", mirror)
    head_rows = jnp.concatenate([result[:tq], back, result[tq:2 * tq]], 0)
    kept = jnp.where(first_core, head_rows[:row_count], head_rows[row_count:])
    sent = jnp.where(first_core, head_rows[row_count:], head_rows[:row_count])
    got = lax.ppermute(sent, "core", swap)
    merged = jnp.where(
        first_core, jnp.concatenate([kept, got], 1), jnp.concatenate([got, kept], 1)
    )
    return merged, early


def pack_attention(
    short_q, short_k, short_v, short_seg, pool_kv, page_table, block_index, block_count
):
    pack_rows, width = short_q.shape
    heads_dev = width // HD
    pool_pages = pool_kv.shape[0]
    page_len = pool_kv.shape[2]
    page_rows = page_table.reshape(block_count, -1)
    entries = page_rows.shape[1]
    capacity = entries // block_count
    owners = page_rows // pool_pages
    places = page_rows % pool_pages
    wanted = owners == block_index
    ranks = jnp.cumsum(wanted.astype(jnp.int32), axis=1) - 1
    picked = wanted[:, :, None] & (
        ranks[:, :, None] == jnp.arange(capacity, dtype=jnp.int32)[None, None, :]
    )
    send_places = jnp.sum(jnp.where(picked, places[:, :, None], 0), axis=1)
    outgoing = pool_kv[send_places.reshape(-1)].reshape(block_count, capacity, 2, page_len, width)
    arrived = lax.all_to_all(outgoing, ("chip", "core"), split_axis=0, concat_axis=0, tiled=True)
    my_owners = lax.dynamic_index_in_dim(owners, block_index, 0, keepdims=False)
    order = jnp.arange(entries, dtype=jnp.int32)
    before = (my_owners[None, :] == my_owners[:, None]) & (order[None, :] < order[:, None])
    slots = my_owners * capacity + jnp.sum(before.astype(jnp.int32), axis=1)
    fetched = arrived.reshape(block_count * capacity, 2, page_len, width)[slots]
    cache_len = entries * page_len
    key_rows = jnp.concatenate([fetched[:, 0].reshape(cache_len, width), short_k], 0)
    value_rows = jnp.concatenate([fetched[:, 1].reshape(cache_len, width), short_v], 0)
    segment = short_seg[0]
    positions = jnp.arange(pack_rows, dtype=jnp.int32)
    key_seg = jnp.concatenate([jnp.arange(cache_len, dtype=jnp.int32) // (PPS * page_len), segment])
    key_pos = jnp.concatenate([jnp.full((cache_len,), -1, jnp.int32), positions])
    allowed = ((key_seg[None, :] == segment[:, None]) & (key_pos[None, :] <= positions[:, None]))[
        None
    ]
    query_heads = short_q.reshape(pack_rows, heads_dev, HD)
    key_heads = key_rows.reshape(cache_len + pack_rows, heads_dev, HD)
    value_heads = value_rows.reshape(cache_len + pack_rows, heads_dev, HD)
    scores = jnp.einsum(
        "qhd,khd->hqk", query_heads, key_heads, preferred_element_type=jnp.float32
    ) * HD ** (-0.5)
    scores = jnp.where(allowed, scores, very_negative)
    row_max = jnp.max(scores, axis=-1)
    weights = jnp.where(allowed, jnp.exp(scores - row_max[..., None]), 0.0)
    total = jnp.sum(weights, axis=-1)
    numer = jnp.einsum(
        "hqk,khd->hqd",
        weights.astype(jnp.bfloat16),
        value_heads,
        preferred_element_type=jnp.float32,
    )
    merged = numer / total[..., None]
    return merged.transpose(1, 0, 2).reshape(pack_rows, width).astype(jnp.bfloat16)


def per_device(
    long_q, long_k, long_v, short_q, short_k, short_v, short_seg, pool_kv, page_table, w_out
):
    block_count = lax.axis_size("chip") * lax.axis_size("core")
    chip = lax.axis_index("chip")
    core = lax.axis_index("core")
    block_index = chip * lax.axis_size("core") + core
    short_attn = pack_attention(
        short_q, short_k, short_v, short_seg, pool_kv, page_table, block_index, block_count
    )
    short_rows = lax.all_to_all(short_attn, "req", 0, 1, tiled=True)
    short_out = jnp.dot(short_rows, w_out, preferred_element_type=jnp.float32).astype(jnp.bfloat16)
    long_attn, short_out = prompt_attention(long_q, long_k, long_v, chip, core, short_out)
    long_rows = lax.all_to_all(long_attn, "req", 0, 1, tiled=True)
    long_out = jnp.dot(long_rows, w_out, preferred_element_type=jnp.float32).astype(jnp.bfloat16)
    return (long_out, short_out)


def solution(mesh):
    chips = mesh.shape["blk"] // 2
    mesh = jax.sharding.Mesh(
        mesh.devices.reshape(chips, 2, mesh.shape["req"]), ("chip", "core", "req")
    )
    blk = ("chip", "core")
    placed = (
        P(blk, "req"),
        P(blk, "req"),
        P(blk, "req"),
        P(blk, "req"),
        P(blk, "req"),
        P(blk, "req"),
        P(blk, None),
        P(blk, None, None, "req"),
        P(),
        P(),
    )
    return jax.shard_map(
        per_device,
        mesh=mesh,
        in_specs=placed,
        out_specs=(P(blk + ("req",), None), P(blk + ("req",), None)),
        check_vma=False,
    )
```

```python
import functools
import math

import jax
import jax.numpy as jnp
from jax import lax
from jax.experimental import pallas as pl
from jax.experimental.pallas import tpu as pltpu
from jax.sharding import PartitionSpec as P

HD = 128
PPS = 4


very_negative = -1e30


def tile_of_step(step, pos_ref):
    q_tile = (step >= pos_ref[2]).astype(jnp.int32)
    return q_tile, step - q_tile * pos_ref[2]


def flash_body(pos_ref, q_ref, k_ref, v_ref, o_ref, m_sc, l_sc, acc_sc, *, heads, tq, tk):
    q_tile, k_tile = tile_of_step(pl.program_id(0), pos_ref)
    first_query = pos_ref[q_tile]
    last_tile = (first_query + tq - 1) // tk

    @pl.when(k_tile == 0)
    def _():
        m_sc[...] = jnp.full(m_sc.shape, very_negative, jnp.float32)
        l_sc[...] = jnp.zeros(l_sc.shape, jnp.float32)
        acc_sc[...] = jnp.zeros(acc_sc.shape, jnp.float32)

    def fold(masked):
        for h in range(heads):
            cols = slice(h * HD, (h + 1) * HD)
            scores = lax.dot_general(
                q_ref[:, cols], k_ref[:, cols], (((1,), (1,)), ((), ())),
                preferred_element_type=jnp.float32,
            ) * HD ** (-0.5)
            if masked:
                query_pos = first_query + lax.broadcasted_iota(jnp.int32, (tq, tk), 0)
                key_pos = k_tile * tk + lax.broadcasted_iota(jnp.int32, (tq, tk), 1)
                scores = jnp.where(key_pos <= query_pos, scores, very_negative)
            run_max = m_sc[h]
            new_max = jnp.maximum(run_max, jnp.max(scores, axis=1, keepdims=True))
            weights = jnp.exp(scores - new_max[:, :1])
            factor = jnp.exp(run_max - new_max)
            l_sc[h] = l_sc[h] * factor + jnp.sum(weights, axis=1, keepdims=True)
            m_sc[h] = new_max
            acc_sc[h] = acc_sc[h] * factor + jnp.dot(
                weights.astype(jnp.bfloat16), v_ref[:, cols], preferred_element_type=jnp.float32
            )

    needs_mask = (k_tile + 1) * tk - 1 > first_query

    @pl.when(jnp.logical_not(needs_mask))
    def _():
        fold(False)

    @pl.when(needs_mask)
    def _():
        fold(True)

    @pl.when(k_tile == last_tile)
    def _():
        for h in range(heads):
            o_ref[:, h * HD:(h + 1) * HD] = (acc_sc[h] / l_sc[h]).astype(o_ref.dtype)


def prompt_attention(queries, block_index, long_k, long_v, early=None):
    row_count, width = queries.shape
    heads_dev = width // HD
    kv_piece = lax.all_gather(jnp.concatenate([long_k, long_v], 1), "blk", axis=0, tiled=True)
    if early is not None:
        kv_piece, early = lax.optimization_barrier((kv_piece, early))
    piece_rows = kv_piece.shape[0]
    block_count = lax.axis_size("blk")
    tq = row_count // 2
    mirror = [(src, block_count - 1 - src) for src in range(block_count)]
    partner_half = lax.ppermute(queries[tq:], "blk", mirror)
    tk = min(row_count, 1024)
    own_first = block_index * row_count
    lent_first = (block_count - 1 - block_index) * row_count + tq
    own_steps = (own_first + tq - 1) // tk + 1
    tile_pos = jnp.stack([own_first, lent_first, own_steps]).astype(jnp.int32)
    step_count = ((block_count - 1) * row_count + 2 * tq - 1) // tk + 2

    def kv_map(column):
        def index(step, pos_ref):
            return (tile_of_step(step, pos_ref)[1], column)

        return index

    def q_map(step, pos_ref):
        return (tile_of_step(step, pos_ref)[0], 0)

    body = functools.partial(flash_body, heads=heads_dev, tq=tq, tk=tk)
    result = pl.pallas_call(
        body,
        out_shape=jax.ShapeDtypeStruct((row_count, width), jnp.bfloat16),
        grid_spec=pltpu.PrefetchScalarGridSpec(
            num_scalar_prefetch=1,
            grid=(step_count,),
            in_specs=[
                pl.BlockSpec((tq, width), q_map),
                pl.BlockSpec((tk, width), kv_map(0)),
                pl.BlockSpec((tk, width), kv_map(1)),
            ],
            out_specs=pl.BlockSpec((tq, width), q_map),
            scratch_shapes=[
                pltpu.VMEM((heads_dev, tq, HD), jnp.float32),
                pltpu.VMEM((heads_dev, tq, HD), jnp.float32),
                pltpu.VMEM((heads_dev, tq, HD), jnp.float32),
            ],
        ),
        compiler_params=pltpu.CompilerParams(dimension_semantics=("arbitrary",)),
    )(tile_pos, jnp.concatenate([queries[:tq], partner_half], 0), kv_piece, kv_piece)
    merged = jnp.concatenate([result[:tq], lax.ppermute(result[tq:], "blk", mirror)], 0)
    return merged, early


def pack_attention(
    short_q, short_k, short_v, short_seg, pool_kv, page_table, block_index, block_count
):
    pack_rows, width = short_q.shape
    heads_dev = width // HD
    pool_pages = pool_kv.shape[0]
    page_len = pool_kv.shape[2]
    page_rows = page_table.reshape(block_count, -1)
    entries = page_rows.shape[1]
    capacity = entries // block_count
    owners = page_rows // pool_pages
    places = page_rows % pool_pages
    wanted = owners == block_index
    ranks = jnp.cumsum(wanted.astype(jnp.int32), axis=1) - 1
    picked = wanted[:, :, None] & (
        ranks[:, :, None] == jnp.arange(capacity, dtype=jnp.int32)[None, None, :]
    )
    send_places = jnp.sum(jnp.where(picked, places[:, :, None], 0), axis=1)
    outgoing = pool_kv[send_places.reshape(-1)].reshape(block_count, capacity, 2, page_len, width)
    arrived = lax.all_to_all(outgoing, "blk", split_axis=0, concat_axis=0, tiled=True)
    my_owners = lax.dynamic_index_in_dim(owners, block_index, 0, keepdims=False)
    order = jnp.arange(entries, dtype=jnp.int32)
    before = (my_owners[None, :] == my_owners[:, None]) & (order[None, :] < order[:, None])
    slots = my_owners * capacity + jnp.sum(before.astype(jnp.int32), axis=1)
    fetched = arrived.reshape(block_count * capacity, 2, page_len, width)[slots]
    cache_len = entries * page_len
    key_rows = jnp.concatenate([fetched[:, 0].reshape(cache_len, width), short_k], 0)
    value_rows = jnp.concatenate([fetched[:, 1].reshape(cache_len, width), short_v], 0)
    segment = short_seg[0]
    positions = jnp.arange(pack_rows, dtype=jnp.int32)
    key_seg = jnp.concatenate([jnp.arange(cache_len, dtype=jnp.int32) // (PPS * page_len), segment])
    key_pos = jnp.concatenate([jnp.full((cache_len,), -1, jnp.int32), positions])
    allowed = ((key_seg[None, :] == segment[:, None]) & (key_pos[None, :] <= positions[:, None]))[
        None
    ]
    query_heads = short_q.reshape(pack_rows, heads_dev, HD)
    key_heads = key_rows.reshape(cache_len + pack_rows, heads_dev, HD)
    value_heads = value_rows.reshape(cache_len + pack_rows, heads_dev, HD)
    scores = jnp.einsum(
        "qhd,khd->hqk", query_heads, key_heads, preferred_element_type=jnp.float32
    ) * HD ** (-0.5)
    scores = jnp.where(allowed, scores, very_negative)
    row_max = jnp.max(scores, axis=-1)
    weights = jnp.where(allowed, jnp.exp(scores - row_max[..., None]), 0.0)
    total = jnp.sum(weights, axis=-1)
    numer = jnp.einsum(
        "hqk,khd->hqd",
        weights.astype(jnp.bfloat16),
        value_heads,
        preferred_element_type=jnp.float32,
    )
    merged = numer / total[..., None]
    return merged.transpose(1, 0, 2).reshape(pack_rows, width).astype(jnp.bfloat16)


def per_device(
    long_q, long_k, long_v, short_q, short_k, short_v, short_seg, pool_kv, page_table, w_out
):
    block_count = lax.axis_size("blk")
    block_index = lax.axis_index("blk")
    short_attn = pack_attention(
        short_q, short_k, short_v, short_seg, pool_kv, page_table, block_index, block_count
    )
    short_rows = lax.all_to_all(short_attn, "req", 0, 1, tiled=True)
    short_out = jnp.dot(short_rows, w_out, preferred_element_type=jnp.float32).astype(jnp.bfloat16)
    long_attn, short_out = prompt_attention(long_q, block_index, long_k, long_v, short_out)
    long_rows = lax.all_to_all(long_attn, "req", 0, 1, tiled=True)
    long_out = jnp.dot(long_rows, w_out, preferred_element_type=jnp.float32).astype(jnp.bfloat16)
    return (long_out, short_out)


def solution(mesh):
    placed = (
        P("blk", "req"),
        P("blk", "req"),
        P("blk", "req"),
        P("blk", "req"),
        P("blk", "req"),
        P("blk", "req"),
        P("blk", None),
        P("blk", None, None, "req"),
        P(),
        P(),
    )
    return jax.shard_map(
        per_device,
        mesh=mesh,
        in_specs=placed,
        out_specs=(P(("blk", "req"), None), P(("blk", "req"), None)),
        check_vma=False,
    )
```

```python
import functools
import math

import jax
import jax.numpy as jnp
from jax import lax
from jax.experimental import pallas as pl
from jax.experimental.pallas import tpu as pltpu
from jax.sharding import PartitionSpec as P

HD = 128
PPS = 4


very_negative = -1e30


def tile_of_step(step, pos_ref):
    q_tile = (step >= pos_ref[2]).astype(jnp.int32)
    return q_tile, step - q_tile * pos_ref[2]


def flash_body(pos_ref, q_ref, k_ref, v_ref, o_ref, m_sc, l_sc, acc_sc, *, heads, tq, tk):
    q_tile, k_tile = tile_of_step(pl.program_id(0), pos_ref)
    first_query = pos_ref[q_tile]
    last_tile = (first_query + tq - 1) // tk

    @pl.when(k_tile == 0)
    def _():
        m_sc[...] = jnp.full(m_sc.shape, very_negative, jnp.float32)
        l_sc[...] = jnp.zeros(l_sc.shape, jnp.float32)
        acc_sc[...] = jnp.zeros(acc_sc.shape, jnp.float32)

    def fold(masked):
        for h in range(heads):
            cols = slice(h * HD, (h + 1) * HD)
            scores = lax.dot_general(
                q_ref[:, cols], k_ref[:, cols], (((1,), (1,)), ((), ())),
                preferred_element_type=jnp.float32,
            ) * HD ** (-0.5)
            if masked:
                query_pos = first_query + lax.broadcasted_iota(jnp.int32, (tq, tk), 0)
                key_pos = k_tile * tk + lax.broadcasted_iota(jnp.int32, (tq, tk), 1)
                scores = jnp.where(key_pos <= query_pos, scores, very_negative)
            run_max = m_sc[h]
            new_max = jnp.maximum(run_max, jnp.max(scores, axis=1, keepdims=True))
            weights = jnp.exp(scores - new_max[:, :1])
            factor = jnp.exp(run_max - new_max)
            l_sc[h] = l_sc[h] * factor + jnp.sum(weights, axis=1, keepdims=True)
            m_sc[h] = new_max
            acc_sc[h] = acc_sc[h] * factor + jnp.dot(
                weights.astype(jnp.bfloat16), v_ref[:, cols], preferred_element_type=jnp.float32
            )

    needs_mask = (k_tile + 1) * tk - 1 > first_query

    @pl.when(jnp.logical_not(needs_mask))
    def _():
        fold(False)

    @pl.when(needs_mask)
    def _():
        fold(True)

    @pl.when(k_tile == last_tile)
    def _():
        for h in range(heads):
            o_ref[:, h * HD:(h + 1) * HD] = (acc_sc[h] / l_sc[h]).astype(o_ref.dtype)


def prompt_attention(queries, block_index, long_k, long_v, early=None):
    row_count, width = queries.shape
    heads_dev = width // HD
    block_count = lax.axis_size("blk")
    spread = jnp.broadcast_to(long_k[None], (block_count,) + long_k.shape)
    key_piece = lax.all_to_all(spread, "blk", 0, 0, tiled=True).reshape(-1, width)
    value_piece = lax.all_gather(long_v, "blk", axis=0, tiled=True)
    if early is not None:
        key_piece, value_piece, early = lax.optimization_barrier((key_piece, value_piece, early))
    tq = row_count // 2
    mirror = [(src, block_count - 1 - src) for src in range(block_count)]
    partner_half = lax.ppermute(queries[tq:], "blk", mirror)
    tk = min(row_count, 1024)
    own_first = block_index * row_count
    lent_first = (block_count - 1 - block_index) * row_count + tq
    own_steps = (own_first + tq - 1) // tk + 1
    tile_pos = jnp.stack([own_first, lent_first, own_steps]).astype(jnp.int32)
    step_count = ((block_count - 1) * row_count + 2 * tq - 1) // tk + 2

    def kv_map(step, pos_ref):
        return (tile_of_step(step, pos_ref)[1], 0)

    def q_map(step, pos_ref):
        return (tile_of_step(step, pos_ref)[0], 0)

    body = functools.partial(flash_body, heads=heads_dev, tq=tq, tk=tk)
    result = pl.pallas_call(
        body,
        out_shape=jax.ShapeDtypeStruct((row_count, width), jnp.bfloat16),
        grid_spec=pltpu.PrefetchScalarGridSpec(
            num_scalar_prefetch=1,
            grid=(step_count,),
            in_specs=[
                pl.BlockSpec((tq, width), q_map),
                pl.BlockSpec((tk, width), kv_map),
                pl.BlockSpec((tk, width), kv_map),
            ],
            out_specs=pl.BlockSpec((tq, width), q_map),
            scratch_shapes=[
                pltpu.VMEM((heads_dev, tq, HD), jnp.float32),
                pltpu.VMEM((heads_dev, tq, HD), jnp.float32),
                pltpu.VMEM((heads_dev, tq, HD), jnp.float32),
            ],
        ),
        compiler_params=pltpu.CompilerParams(dimension_semantics=("arbitrary",)),
    )(tile_pos, jnp.concatenate([queries[:tq], partner_half], 0), key_piece, value_piece)
    merged = jnp.concatenate([result[:tq], lax.ppermute(result[tq:], "blk", mirror)], 0)
    return merged, early


def pack_attention(
    short_q, short_k, short_v, short_seg, pool_kv, page_table, block_index, block_count
):
    pack_rows, width = short_q.shape
    heads_dev = width // HD
    pool_pages = pool_kv.shape[0]
    page_len = pool_kv.shape[2]
    page_rows = page_table.reshape(block_count, -1)
    entries = page_rows.shape[1]
    capacity = entries // block_count
    owners = page_rows // pool_pages
    places = page_rows % pool_pages
    wanted = owners == block_index
    ranks = jnp.cumsum(wanted.astype(jnp.int32), axis=1) - 1
    picked = wanted[:, :, None] & (
        ranks[:, :, None] == jnp.arange(capacity, dtype=jnp.int32)[None, None, :]
    )
    send_places = jnp.sum(jnp.where(picked, places[:, :, None], 0), axis=1)
    outgoing = pool_kv[send_places.reshape(-1)].reshape(block_count, capacity, 2, page_len, width)
    arrived = lax.all_to_all(outgoing, "blk", split_axis=0, concat_axis=0, tiled=True)
    my_owners = lax.dynamic_index_in_dim(owners, block_index, 0, keepdims=False)
    order = jnp.arange(entries, dtype=jnp.int32)
    before = (my_owners[None, :] == my_owners[:, None]) & (order[None, :] < order[:, None])
    slots = my_owners * capacity + jnp.sum(before.astype(jnp.int32), axis=1)
    fetched = arrived.reshape(block_count * capacity, 2, page_len, width)[slots]
    cache_len = entries * page_len
    key_rows = jnp.concatenate([fetched[:, 0].reshape(cache_len, width), short_k], 0)
    value_rows = jnp.concatenate([fetched[:, 1].reshape(cache_len, width), short_v], 0)
    segment = short_seg[0]
    positions = jnp.arange(pack_rows, dtype=jnp.int32)
    key_seg = jnp.concatenate([jnp.arange(cache_len, dtype=jnp.int32) // (PPS * page_len), segment])
    key_pos = jnp.concatenate([jnp.full((cache_len,), -1, jnp.int32), positions])
    allowed = ((key_seg[None, :] == segment[:, None]) & (key_pos[None, :] <= positions[:, None]))[
        None
    ]
    query_heads = short_q.reshape(pack_rows, heads_dev, HD)
    key_heads = key_rows.reshape(cache_len + pack_rows, heads_dev, HD)
    value_heads = value_rows.reshape(cache_len + pack_rows, heads_dev, HD)
    scores = jnp.einsum(
        "qhd,khd->hqk", query_heads, key_heads, preferred_element_type=jnp.float32
    ) * HD ** (-0.5)
    scores = jnp.where(allowed, scores, very_negative)
    row_max = jnp.max(scores, axis=-1)
    weights = jnp.where(allowed, jnp.exp(scores - row_max[..., None]), 0.0)
    total = jnp.sum(weights, axis=-1)
    numer = jnp.einsum(
        "hqk,khd->hqd",
        weights.astype(jnp.bfloat16),
        value_heads,
        preferred_element_type=jnp.float32,
    )
    merged = numer / total[..., None]
    return merged.transpose(1, 0, 2).reshape(pack_rows, width).astype(jnp.bfloat16)


def per_device(
    long_q, long_k, long_v, short_q, short_k, short_v, short_seg, pool_kv, page_table, w_out
):
    block_count = lax.axis_size("blk")
    block_index = lax.axis_index("blk")
    short_attn = pack_attention(
        short_q, short_k, short_v, short_seg, pool_kv, page_table, block_index, block_count
    )
    short_rows = lax.all_to_all(short_attn, "req", 0, 1, tiled=True)
    short_out = jnp.dot(short_rows, w_out, preferred_element_type=jnp.float32).astype(jnp.bfloat16)
    long_attn, short_out = prompt_attention(long_q, block_index, long_k, long_v, short_out)
    long_rows = lax.all_to_all(long_attn, "req", 0, 1, tiled=True)
    long_out = jnp.dot(long_rows, w_out, preferred_element_type=jnp.float32).astype(jnp.bfloat16)
    return (long_out, short_out)


def solution(mesh):
    placed = (
        P("blk", "req"),
        P("blk", "req"),
        P("blk", "req"),
        P("blk", "req"),
        P("blk", "req"),
        P("blk", "req"),
        P("blk", None),
        P("blk", None, None, "req"),
        P(),
        P(),
    )
    return jax.shard_map(
        per_device,
        mesh=mesh,
        in_specs=placed,
        out_specs=(P(("blk", "req"), None), P(("blk", "req"), None)),
        check_vma=False,
    )
```

```python
import functools
import math

import jax
import jax.numpy as jnp
from jax import lax
from jax.experimental import pallas as pl
from jax.experimental.pallas import tpu as pltpu
from jax.sharding import PartitionSpec as P

HD = 128
PPS = 4


very_negative = -1e30


def tile_of_step(step, pos_ref):
    q_tile = (step >= pos_ref[2]).astype(jnp.int32)
    return q_tile, step - q_tile * pos_ref[2]


def flash_body(pos_ref, q_ref, k_ref, v_ref, o_ref, m_sc, l_sc, acc_sc, *, heads, tq, tk):
    q_tile, k_tile = tile_of_step(pl.program_id(0), pos_ref)
    first_query = pos_ref[q_tile]
    last_tile = (first_query + tq - 1) // tk

    @pl.when(k_tile == 0)
    def _():
        m_sc[...] = jnp.full(m_sc.shape, very_negative, jnp.float32)
        l_sc[...] = jnp.zeros(l_sc.shape, jnp.float32)
        acc_sc[...] = jnp.zeros(acc_sc.shape, jnp.float32)

    def fold(masked):
        for h in range(heads):
            cols = slice(h * HD, (h + 1) * HD)
            scores = lax.dot_general(
                k_ref[:, cols], q_ref[:, cols], (((1,), (1,)), ((), ())),
                preferred_element_type=jnp.float32,
            ) * HD ** (-0.5)
            if masked:
                key_pos = k_tile * tk + lax.broadcasted_iota(jnp.int32, (tk, tq), 0)
                query_pos = first_query + lax.broadcasted_iota(jnp.int32, (tk, tq), 1)
                scores = jnp.where(key_pos <= query_pos, scores, very_negative)
            run_max = m_sc[h]
            new_max = jnp.maximum(run_max, jnp.max(scores, axis=0, keepdims=True))
            weights = jnp.exp(scores - new_max)
            factor = jnp.exp(run_max - new_max)
            l_sc[h] = l_sc[h] * factor + jnp.sum(weights, axis=0, keepdims=True)
            m_sc[h] = new_max
            acc_sc[h] = acc_sc[h] * factor + lax.dot_general(
                v_ref[:, cols], weights.astype(jnp.bfloat16), (((0,), (0,)), ((), ())),
                preferred_element_type=jnp.float32,
            )

    needs_mask = (k_tile + 1) * tk - 1 > first_query

    @pl.when(jnp.logical_not(needs_mask))
    def _():
        fold(False)

    @pl.when(needs_mask)
    def _():
        fold(True)

    @pl.when(k_tile == last_tile)
    def _():
        for h in range(heads):
            o_ref[:, h * HD:(h + 1) * HD] = (acc_sc[h] / l_sc[h]).T.astype(o_ref.dtype)


def prompt_attention(queries, block_index, long_k, long_v, early=None):
    row_count, width = queries.shape
    heads_dev = width // HD
    kv_piece = lax.all_gather(jnp.concatenate([long_k, long_v], 1), "blk", axis=0, tiled=True)
    if early is not None:
        kv_piece, early = lax.optimization_barrier((kv_piece, early))
    piece_rows = kv_piece.shape[0]
    block_count = lax.axis_size("blk")
    tq = row_count // 2
    mirror = [(src, block_count - 1 - src) for src in range(block_count)]
    partner_half = lax.ppermute(queries[tq:], "blk", mirror)
    tk = min(row_count, 1024)
    own_first = block_index * row_count
    lent_first = (block_count - 1 - block_index) * row_count + tq
    own_steps = (own_first + tq - 1) // tk + 1
    tile_pos = jnp.stack([own_first, lent_first, own_steps]).astype(jnp.int32)
    step_count = ((block_count - 1) * row_count + 2 * tq - 1) // tk + 2

    def kv_map(column):
        def index(step, pos_ref):
            return (tile_of_step(step, pos_ref)[1], column)

        return index

    def q_map(step, pos_ref):
        return (tile_of_step(step, pos_ref)[0], 0)

    body = functools.partial(flash_body, heads=heads_dev, tq=tq, tk=tk)
    result = pl.pallas_call(
        body,
        out_shape=jax.ShapeDtypeStruct((row_count, width), jnp.bfloat16),
        grid_spec=pltpu.PrefetchScalarGridSpec(
            num_scalar_prefetch=1,
            grid=(step_count,),
            in_specs=[
                pl.BlockSpec((tq, width), q_map),
                pl.BlockSpec((tk, width), kv_map(0)),
                pl.BlockSpec((tk, width), kv_map(1)),
            ],
            out_specs=pl.BlockSpec((tq, width), q_map),
            scratch_shapes=[
                pltpu.VMEM((heads_dev, 1, tq), jnp.float32),
                pltpu.VMEM((heads_dev, 1, tq), jnp.float32),
                pltpu.VMEM((heads_dev, HD, tq), jnp.float32),
            ],
        ),
        compiler_params=pltpu.CompilerParams(dimension_semantics=("arbitrary",)),
    )(tile_pos, jnp.concatenate([queries[:tq], partner_half], 0), kv_piece, kv_piece)
    merged = jnp.concatenate([result[:tq], lax.ppermute(result[tq:], "blk", mirror)], 0)
    return merged, early


def pack_attention(
    short_q, short_k, short_v, short_seg, pool_kv, page_table, block_index, block_count
):
    pack_rows, width = short_q.shape
    heads_dev = width // HD
    pool_pages = pool_kv.shape[0]
    page_len = pool_kv.shape[2]
    page_rows = page_table.reshape(block_count, -1)
    entries = page_rows.shape[1]
    capacity = entries // block_count
    owners = page_rows // pool_pages
    places = page_rows % pool_pages
    wanted = owners == block_index
    ranks = jnp.cumsum(wanted.astype(jnp.int32), axis=1) - 1
    picked = wanted[:, :, None] & (
        ranks[:, :, None] == jnp.arange(capacity, dtype=jnp.int32)[None, None, :]
    )
    send_places = jnp.sum(jnp.where(picked, places[:, :, None], 0), axis=1)
    outgoing = pool_kv[send_places.reshape(-1)].reshape(block_count, capacity, 2, page_len, width)
    arrived = lax.all_to_all(outgoing, "blk", split_axis=0, concat_axis=0, tiled=True)
    my_owners = lax.dynamic_index_in_dim(owners, block_index, 0, keepdims=False)
    order = jnp.arange(entries, dtype=jnp.int32)
    before = (my_owners[None, :] == my_owners[:, None]) & (order[None, :] < order[:, None])
    slots = my_owners * capacity + jnp.sum(before.astype(jnp.int32), axis=1)
    fetched = arrived.reshape(block_count * capacity, 2, page_len, width)[slots]
    cache_len = entries * page_len
    key_rows = jnp.concatenate([fetched[:, 0].reshape(cache_len, width), short_k], 0)
    value_rows = jnp.concatenate([fetched[:, 1].reshape(cache_len, width), short_v], 0)
    segment = short_seg[0]
    positions = jnp.arange(pack_rows, dtype=jnp.int32)
    key_seg = jnp.concatenate([jnp.arange(cache_len, dtype=jnp.int32) // (PPS * page_len), segment])
    key_pos = jnp.concatenate([jnp.full((cache_len,), -1, jnp.int32), positions])
    allowed = ((key_seg[None, :] == segment[:, None]) & (key_pos[None, :] <= positions[:, None]))[
        None
    ]
    query_heads = short_q.reshape(pack_rows, heads_dev, HD)
    key_heads = key_rows.reshape(cache_len + pack_rows, heads_dev, HD)
    value_heads = value_rows.reshape(cache_len + pack_rows, heads_dev, HD)
    scores = jnp.einsum(
        "qhd,khd->hqk", query_heads, key_heads, preferred_element_type=jnp.float32
    ) * HD ** (-0.5)
    scores = jnp.where(allowed, scores, very_negative)
    row_max = jnp.max(scores, axis=-1)
    weights = jnp.where(allowed, jnp.exp(scores - row_max[..., None]), 0.0)
    total = jnp.sum(weights, axis=-1)
    numer = jnp.einsum(
        "hqk,khd->hqd",
        weights.astype(jnp.bfloat16),
        value_heads,
        preferred_element_type=jnp.float32,
    )
    merged = numer / total[..., None]
    return merged.transpose(1, 0, 2).reshape(pack_rows, width).astype(jnp.bfloat16)


def per_device(
    long_q, long_k, long_v, short_q, short_k, short_v, short_seg, pool_kv, page_table, w_out
):
    block_count = lax.axis_size("blk")
    block_index = lax.axis_index("blk")
    short_attn = pack_attention(
        short_q, short_k, short_v, short_seg, pool_kv, page_table, block_index, block_count
    )
    short_rows = lax.all_to_all(short_attn, "req", 0, 1, tiled=True)
    short_out = jnp.dot(short_rows, w_out, preferred_element_type=jnp.float32).astype(jnp.bfloat16)
    long_attn, short_out = prompt_attention(long_q, block_index, long_k, long_v, short_out)
    long_rows = lax.all_to_all(long_attn, "req", 0, 1, tiled=True)
    long_out = jnp.dot(long_rows, w_out, preferred_element_type=jnp.float32).astype(jnp.bfloat16)
    return (long_out, short_out)


def solution(mesh):
    placed = (
        P("blk", "req"),
        P("blk", "req"),
        P("blk", "req"),
        P("blk", "req"),
        P("blk", "req"),
        P("blk", "req"),
        P("blk", None),
        P("blk", None, None, "req"),
        P(),
        P(),
    )
    return jax.shard_map(
        per_device,
        mesh=mesh,
        in_specs=placed,
        out_specs=(P(("blk", "req"), None), P(("blk", "req"), None)),
        check_vma=False,
    )
```

```python
import functools
import math

import jax
import jax.numpy as jnp
from jax import lax
from jax.experimental import pallas as pl
from jax.experimental.pallas import tpu as pltpu
from jax.sharding import PartitionSpec as P

HD = 128
PPS = 4


very_negative = -1e30


def tile_of_step(step, pos_ref):
    q_tile = (step >= pos_ref[2]).astype(jnp.int32)
    return q_tile, step - q_tile * pos_ref[2]


def flash_body(pos_ref, q_ref, k_ref, v_ref, o_ref, m_sc, l_sc, acc_sc, *, heads, tq, tk):
    q_tile, k_tile = tile_of_step(pl.program_id(0), pos_ref)
    first_query = pos_ref[q_tile]
    last_tile = (first_query + tq - 1) // tk

    @pl.when(k_tile == 0)
    def _():
        m_sc[...] = jnp.full(m_sc.shape, very_negative, jnp.float32)
        l_sc[...] = jnp.zeros(l_sc.shape, jnp.float32)
        acc_sc[...] = jnp.zeros(acc_sc.shape, jnp.float32)

    def fold(masked):
        for h in range(heads):
            cols = slice(h * HD, (h + 1) * HD)
            scores = lax.dot_general(
                k_ref[:, cols], q_ref[:, cols], (((1,), (1,)), ((), ())),
                preferred_element_type=jnp.float32,
            ) * HD ** (-0.5)
            if masked:
                key_pos = k_tile * tk + lax.broadcasted_iota(jnp.int32, (tk, tq), 0)
                query_pos = first_query + lax.broadcasted_iota(jnp.int32, (tk, tq), 1)
                scores = jnp.where(key_pos <= query_pos, scores, very_negative)
            run_max = m_sc[h]
            new_max = jnp.maximum(run_max, jnp.max(scores, axis=0, keepdims=True))
            weights = jnp.exp(scores - new_max)
            factor = jnp.exp(run_max - new_max)
            l_sc[h] = l_sc[h] * factor + jnp.sum(weights, axis=0, keepdims=True)
            m_sc[h] = new_max
            acc_sc[h] = acc_sc[h] * factor + lax.dot_general(
                v_ref[:, cols], weights.astype(jnp.bfloat16), (((0,), (0,)), ((), ())),
                preferred_element_type=jnp.float32,
            )

    needs_mask = (k_tile + 1) * tk - 1 > first_query

    @pl.when(jnp.logical_not(needs_mask))
    def _():
        fold(False)

    @pl.when(needs_mask)
    def _():
        fold(True)

    @pl.when(k_tile == last_tile)
    def _():
        for h in range(heads):
            o_ref[:, h * HD:(h + 1) * HD] = (acc_sc[h] / l_sc[h]).T.astype(o_ref.dtype)


def prompt_attention(queries, block_index, long_k, long_v, early=None):
    row_count, width = queries.shape
    heads_dev = width // HD
    kv_piece = lax.all_gather(jnp.concatenate([long_k, long_v], 1), "blk", axis=0, tiled=True)
    if early is not None:
        kv_piece, early = lax.optimization_barrier((kv_piece, early))
    piece_rows = kv_piece.shape[0]
    block_count = lax.axis_size("blk")
    tq = row_count // 2
    mirror = [(src, block_count - 1 - src) for src in range(block_count)]
    partner_half = lax.ppermute(queries[tq:], "blk", mirror)
    tk = min(piece_rows, 2 * row_count)
    own_first = block_index * row_count
    lent_first = (block_count - 1 - block_index) * row_count + tq
    own_steps = (own_first + tq - 1) // tk + 1
    tile_pos = jnp.stack([own_first, lent_first, own_steps]).astype(jnp.int32)
    counts = {
        (d * row_count + tq - 1) // tk + ((block_count - 1 - d) * row_count + 2 * tq - 1) // tk + 2
        for d in range(block_count)
    }
    assert len(counts) == 1
    step_count = counts.pop()

    def kv_map(column):
        def index(step, pos_ref):
            return (tile_of_step(step, pos_ref)[1], column)

        return index

    def q_map(step, pos_ref):
        return (tile_of_step(step, pos_ref)[0], 0)

    body = functools.partial(flash_body, heads=heads_dev, tq=tq, tk=tk)
    result = pl.pallas_call(
        body,
        out_shape=jax.ShapeDtypeStruct((row_count, width), jnp.bfloat16),
        grid_spec=pltpu.PrefetchScalarGridSpec(
            num_scalar_prefetch=1,
            grid=(step_count,),
            in_specs=[
                pl.BlockSpec((tq, width), q_map),
                pl.BlockSpec((tk, width), kv_map(0)),
                pl.BlockSpec((tk, width), kv_map(1)),
            ],
            out_specs=pl.BlockSpec((tq, width), q_map),
            scratch_shapes=[
                pltpu.VMEM((heads_dev, 1, tq), jnp.float32),
                pltpu.VMEM((heads_dev, 1, tq), jnp.float32),
                pltpu.VMEM((heads_dev, HD, tq), jnp.float32),
            ],
        ),
        compiler_params=pltpu.CompilerParams(dimension_semantics=("arbitrary",)),
    )(tile_pos, jnp.concatenate([queries[:tq], partner_half], 0), kv_piece, kv_piece)
    merged = jnp.concatenate([result[:tq], lax.ppermute(result[tq:], "blk", mirror)], 0)
    return merged, early


def pack_attention(
    short_q, short_k, short_v, short_seg, pool_kv, page_table, block_index, block_count
):
    pack_rows, width = short_q.shape
    heads_dev = width // HD
    pool_pages = pool_kv.shape[0]
    page_len = pool_kv.shape[2]
    page_rows = page_table.reshape(block_count, -1)
    entries = page_rows.shape[1]
    capacity = entries // block_count
    owners = page_rows // pool_pages
    places = page_rows % pool_pages
    wanted = owners == block_index
    ranks = jnp.cumsum(wanted.astype(jnp.int32), axis=1) - 1
    picked = wanted[:, :, None] & (
        ranks[:, :, None] == jnp.arange(capacity, dtype=jnp.int32)[None, None, :]
    )
    send_places = jnp.sum(jnp.where(picked, places[:, :, None], 0), axis=1)
    outgoing = pool_kv[send_places.reshape(-1)].reshape(block_count, capacity, 2, page_len, width)
    arrived = lax.all_to_all(outgoing, "blk", split_axis=0, concat_axis=0, tiled=True)
    my_owners = lax.dynamic_index_in_dim(owners, block_index, 0, keepdims=False)
    order = jnp.arange(entries, dtype=jnp.int32)
    before = (my_owners[None, :] == my_owners[:, None]) & (order[None, :] < order[:, None])
    slots = my_owners * capacity + jnp.sum(before.astype(jnp.int32), axis=1)
    fetched = arrived.reshape(block_count * capacity, 2, page_len, width)[slots]
    cache_len = entries * page_len
    key_rows = jnp.concatenate([fetched[:, 0].reshape(cache_len, width), short_k], 0)
    value_rows = jnp.concatenate([fetched[:, 1].reshape(cache_len, width), short_v], 0)
    segment = short_seg[0]
    positions = jnp.arange(pack_rows, dtype=jnp.int32)
    key_seg = jnp.concatenate([jnp.arange(cache_len, dtype=jnp.int32) // (PPS * page_len), segment])
    key_pos = jnp.concatenate([jnp.full((cache_len,), -1, jnp.int32), positions])
    allowed = ((key_seg[None, :] == segment[:, None]) & (key_pos[None, :] <= positions[:, None]))[
        None
    ]
    query_heads = short_q.reshape(pack_rows, heads_dev, HD)
    key_heads = key_rows.reshape(cache_len + pack_rows, heads_dev, HD)
    value_heads = value_rows.reshape(cache_len + pack_rows, heads_dev, HD)
    scores = jnp.einsum(
        "qhd,khd->hqk", query_heads, key_heads, preferred_element_type=jnp.float32
    ) * HD ** (-0.5)
    scores = jnp.where(allowed, scores, very_negative)
    row_max = jnp.max(scores, axis=-1)
    weights = jnp.where(allowed, jnp.exp(scores - row_max[..., None]), 0.0)
    total = jnp.sum(weights, axis=-1)
    numer = jnp.einsum(
        "hqk,khd->hqd",
        weights.astype(jnp.bfloat16),
        value_heads,
        preferred_element_type=jnp.float32,
    )
    merged = numer / total[..., None]
    return merged.transpose(1, 0, 2).reshape(pack_rows, width).astype(jnp.bfloat16)


def per_device(
    long_q, long_k, long_v, short_q, short_k, short_v, short_seg, pool_kv, page_table, w_out
):
    block_count = lax.axis_size("blk")
    block_index = lax.axis_index("blk")
    short_attn = pack_attention(
        short_q, short_k, short_v, short_seg, pool_kv, page_table, block_index, block_count
    )
    short_rows = lax.all_to_all(short_attn, "req", 0, 1, tiled=True)
    short_out = jnp.dot(short_rows, w_out, preferred_element_type=jnp.float32).astype(jnp.bfloat16)
    long_attn, short_out = prompt_attention(long_q, block_index, long_k, long_v, short_out)
    long_rows = lax.all_to_all(long_attn, "req", 0, 1, tiled=True)
    long_out = jnp.dot(long_rows, w_out, preferred_element_type=jnp.float32).astype(jnp.bfloat16)
    return (long_out, short_out)


def solution(mesh):
    placed = (
        P("blk", "req"),
        P("blk", "req"),
        P("blk", "req"),
        P("blk", "req"),
        P("blk", "req"),
        P("blk", "req"),
        P("blk", None),
        P("blk", None, None, "req"),
        P(),
        P(),
    )
    return jax.shard_map(
        per_device,
        mesh=mesh,
        in_specs=placed,
        out_specs=(P(("blk", "req"), None), P(("blk", "req"), None)),
        check_vma=False,
    )
```

```python
import functools
import math

import jax
import jax.numpy as jnp
from jax import lax
from jax.experimental import pallas as pl
from jax.experimental.pallas import tpu as pltpu
from jax.sharding import PartitionSpec as P

HD = 128
PPS = 4


very_negative = -1e30


def tile_of_step(step, pos_ref):
    q_tile = (step >= pos_ref[2]).astype(jnp.int32)
    return q_tile, step - q_tile * pos_ref[2]


def flash_body(pos_ref, q_ref, k_ref, v_ref, o_ref, m_sc, l_sc, acc_sc, *, heads, tq, tk):
    q_tile, k_tile = tile_of_step(pl.program_id(0), pos_ref)
    first_query = pos_ref[q_tile]
    last_tile = (first_query + tq - 1) // tk

    @pl.when(k_tile == 0)
    def _():
        m_sc[...] = jnp.full(m_sc.shape, very_negative, jnp.float32)
        l_sc[...] = jnp.zeros(l_sc.shape, jnp.float32)
        acc_sc[...] = jnp.zeros(acc_sc.shape, jnp.float32)

    def fold(masked):
        for h in range(heads):
            cols = slice(h * HD, (h + 1) * HD)
            scores = lax.dot_general(
                k_ref[:, cols], q_ref[:, cols], (((1,), (1,)), ((), ())),
                preferred_element_type=jnp.float32,
            ) * HD ** (-0.5)
            if masked:
                key_pos = k_tile * tk + lax.broadcasted_iota(jnp.int32, (tk, tq), 0)
                query_pos = first_query + lax.broadcasted_iota(jnp.int32, (tk, tq), 1)
                scores = jnp.where(key_pos <= query_pos, scores, very_negative)
            run_max = m_sc[h]
            new_max = jnp.maximum(run_max, jnp.max(scores, axis=0, keepdims=True))
            weights = jnp.exp(scores - new_max)
            factor = jnp.exp(run_max - new_max)
            l_sc[h] = l_sc[h] * factor + jnp.sum(weights, axis=0, keepdims=True)
            m_sc[h] = new_max
            acc_sc[h] = acc_sc[h] * factor + lax.dot_general(
                v_ref[:, cols], weights.astype(jnp.bfloat16), (((0,), (0,)), ((), ())),
                preferred_element_type=jnp.float32,
            )

    needs_mask = (k_tile + 1) * tk - 1 > first_query

    @pl.when(jnp.logical_not(needs_mask))
    def _():
        fold(False)

    @pl.when(needs_mask)
    def _():
        fold(True)

    @pl.when(k_tile == last_tile)
    def _():
        for h in range(heads):
            o_ref[:, h * HD:(h + 1) * HD] = (acc_sc[h] / l_sc[h]).T.astype(o_ref.dtype)


def prompt_attention(queries, block_index, long_k, long_v, early=None):
    row_count, width = queries.shape
    heads_dev = width // HD
    kv_piece = lax.all_gather(jnp.concatenate([long_k, long_v], 1), "blk", axis=0, tiled=True)
    if early is not None:
        kv_piece, early = lax.optimization_barrier((kv_piece, early))
    piece_rows = kv_piece.shape[0]
    block_count = lax.axis_size("blk")
    tq = row_count // 2
    chip_count = block_count // 2
    mirror = [(src, 2 * (chip_count - 1 - src // 2) + src % 2) for src in range(block_count)]
    partner_block = 2 * (chip_count - 1 - block_index // 2) + block_index % 2
    partner_half = lax.ppermute(queries[tq:], "blk", mirror)
    tk = min(piece_rows, 2 * row_count)
    own_first = block_index * row_count
    lent_first = partner_block * row_count + tq
    own_steps = (own_first + tq - 1) // tk + 1
    tile_pos = jnp.stack([own_first, lent_first, own_steps]).astype(jnp.int32)
    counts = {
        (d * row_count + tq - 1) // tk + (dict(mirror)[d] * row_count + 2 * tq - 1) // tk + 2
        for d in range(block_count)
    }
    assert len(counts) == 1
    step_count = counts.pop()

    def kv_map(column):
        def index(step, pos_ref):
            return (tile_of_step(step, pos_ref)[1], column)

        return index

    def q_map(step, pos_ref):
        return (tile_of_step(step, pos_ref)[0], 0)

    body = functools.partial(flash_body, heads=heads_dev, tq=tq, tk=tk)
    result = pl.pallas_call(
        body,
        out_shape=jax.ShapeDtypeStruct((row_count, width), jnp.bfloat16),
        grid_spec=pltpu.PrefetchScalarGridSpec(
            num_scalar_prefetch=1,
            grid=(step_count,),
            in_specs=[
                pl.BlockSpec((tq, width), q_map),
                pl.BlockSpec((tk, width), kv_map(0)),
                pl.BlockSpec((tk, width), kv_map(1)),
            ],
            out_specs=pl.BlockSpec((tq, width), q_map),
            scratch_shapes=[
                pltpu.VMEM((heads_dev, 1, tq), jnp.float32),
                pltpu.VMEM((heads_dev, 1, tq), jnp.float32),
                pltpu.VMEM((heads_dev, HD, tq), jnp.float32),
            ],
        ),
        compiler_params=pltpu.CompilerParams(dimension_semantics=("arbitrary",)),
    )(tile_pos, jnp.concatenate([queries[:tq], partner_half], 0), kv_piece, kv_piece)
    merged = jnp.concatenate([result[:tq], lax.ppermute(result[tq:], "blk", mirror)], 0)
    return merged, early


def pack_attention(
    short_q, short_k, short_v, short_seg, pool_kv, page_table, block_index, block_count
):
    pack_rows, width = short_q.shape
    heads_dev = width // HD
    pool_pages = pool_kv.shape[0]
    page_len = pool_kv.shape[2]
    page_rows = page_table.reshape(block_count, -1)
    entries = page_rows.shape[1]
    capacity = entries // block_count
    owners = page_rows // pool_pages
    places = page_rows % pool_pages
    wanted = owners == block_index
    ranks = jnp.cumsum(wanted.astype(jnp.int32), axis=1) - 1
    picked = wanted[:, :, None] & (
        ranks[:, :, None] == jnp.arange(capacity, dtype=jnp.int32)[None, None, :]
    )
    send_places = jnp.sum(jnp.where(picked, places[:, :, None], 0), axis=1)
    outgoing = pool_kv[send_places.reshape(-1)].reshape(block_count, capacity, 2, page_len, width)
    arrived = lax.all_to_all(outgoing, "blk", split_axis=0, concat_axis=0, tiled=True)
    my_owners = lax.dynamic_index_in_dim(owners, block_index, 0, keepdims=False)
    order = jnp.arange(entries, dtype=jnp.int32)
    before = (my_owners[None, :] == my_owners[:, None]) & (order[None, :] < order[:, None])
    slots = my_owners * capacity + jnp.sum(before.astype(jnp.int32), axis=1)
    fetched = arrived.reshape(block_count * capacity, 2, page_len, width)[slots]
    cache_len = entries * page_len
    key_rows = jnp.concatenate([fetched[:, 0].reshape(cache_len, width), short_k], 0)
    value_rows = jnp.concatenate([fetched[:, 1].reshape(cache_len, width), short_v], 0)
    segment = short_seg[0]
    positions = jnp.arange(pack_rows, dtype=jnp.int32)
    key_seg = jnp.concatenate([jnp.arange(cache_len, dtype=jnp.int32) // (PPS * page_len), segment])
    key_pos = jnp.concatenate([jnp.full((cache_len,), -1, jnp.int32), positions])
    allowed = ((key_seg[None, :] == segment[:, None]) & (key_pos[None, :] <= positions[:, None]))[
        None
    ]
    query_heads = short_q.reshape(pack_rows, heads_dev, HD)
    key_heads = key_rows.reshape(cache_len + pack_rows, heads_dev, HD)
    value_heads = value_rows.reshape(cache_len + pack_rows, heads_dev, HD)
    scores = jnp.einsum(
        "qhd,khd->hqk", query_heads, key_heads, preferred_element_type=jnp.float32
    ) * HD ** (-0.5)
    scores = jnp.where(allowed, scores, very_negative)
    row_max = jnp.max(scores, axis=-1)
    weights = jnp.where(allowed, jnp.exp(scores - row_max[..., None]), 0.0)
    total = jnp.sum(weights, axis=-1)
    numer = jnp.einsum(
        "hqk,khd->hqd",
        weights.astype(jnp.bfloat16),
        value_heads,
        preferred_element_type=jnp.float32,
    )
    merged = numer / total[..., None]
    return merged.transpose(1, 0, 2).reshape(pack_rows, width).astype(jnp.bfloat16)


def per_device(
    long_q, long_k, long_v, short_q, short_k, short_v, short_seg, pool_kv, page_table, w_out
):
    block_count = lax.axis_size("blk")
    block_index = lax.axis_index("blk")
    short_attn = pack_attention(
        short_q, short_k, short_v, short_seg, pool_kv, page_table, block_index, block_count
    )
    short_rows = lax.all_to_all(short_attn, "req", 0, 1, tiled=True)
    short_out = jnp.dot(short_rows, w_out, preferred_element_type=jnp.float32).astype(jnp.bfloat16)
    long_attn, short_out = prompt_attention(long_q, block_index, long_k, long_v, short_out)
    long_rows = lax.all_to_all(long_attn, "req", 0, 1, tiled=True)
    long_out = jnp.dot(long_rows, w_out, preferred_element_type=jnp.float32).astype(jnp.bfloat16)
    return (long_out, short_out)


def solution(mesh):
    placed = (
        P("blk", "req"),
        P("blk", "req"),
        P("blk", "req"),
        P("blk", "req"),
        P("blk", "req"),
        P("blk", "req"),
        P("blk", None),
        P("blk", None, None, "req"),
        P(),
        P(),
    )
    return jax.shard_map(
        per_device,
        mesh=mesh,
        in_specs=placed,
        out_specs=(P(("blk", "req"), None), P(("blk", "req"), None)),
        check_vma=False,
    )
```

```python
import functools
import math

import jax
import jax.numpy as jnp
from jax import lax
from jax.experimental import pallas as pl
from jax.experimental.pallas import tpu as pltpu
from jax.sharding import PartitionSpec as P

HD = 128
PPS = 4


very_negative = -1e30


def tile_of_step(step, pos_ref):
    q_tile = (step >= pos_ref[2]).astype(jnp.int32)
    return q_tile, step - q_tile * pos_ref[2]


def flash_body(pos_ref, q_ref, k_ref, v_ref, o_ref, m_sc, l_sc, acc_sc, *, heads, tq, tk):
    q_tile, k_tile = tile_of_step(pl.program_id(0), pos_ref)
    first_query = pos_ref[q_tile]
    last_tile = (first_query + tq - 1) // tk

    @pl.when(k_tile == 0)
    def _():
        m_sc[...] = jnp.full(m_sc.shape, very_negative, jnp.float32)
        l_sc[...] = jnp.zeros(l_sc.shape, jnp.float32)
        acc_sc[...] = jnp.zeros(acc_sc.shape, jnp.float32)

    def fold(masked):
        for h in range(heads):
            cols = slice(h * HD, (h + 1) * HD)
            scores = lax.dot_general(
                k_ref[:, cols], q_ref[:, cols], (((1,), (1,)), ((), ())),
                preferred_element_type=jnp.float32,
            ) * HD ** (-0.5)
            if masked:
                key_pos = k_tile * tk + lax.broadcasted_iota(jnp.int32, (tk, tq), 0)
                query_pos = first_query + lax.broadcasted_iota(jnp.int32, (tk, tq), 1)
                scores = jnp.where(key_pos <= query_pos, scores, very_negative)
            run_max = m_sc[h]
            new_max = jnp.maximum(run_max, jnp.max(scores, axis=0, keepdims=True))
            weights = jnp.exp(scores - new_max)
            factor = jnp.exp(run_max - new_max)
            l_sc[h] = l_sc[h] * factor + jnp.sum(weights, axis=0, keepdims=True)
            m_sc[h] = new_max
            acc_sc[h] = acc_sc[h] * factor + lax.dot_general(
                v_ref[:, cols], weights.astype(jnp.bfloat16), (((0,), (0,)), ((), ())),
                preferred_element_type=jnp.float32,
            )

    needs_mask = (k_tile + 1) * tk - 1 > first_query

    @pl.when(jnp.logical_not(needs_mask))
    def _():
        fold(False)

    @pl.when(needs_mask)
    def _():
        fold(True)

    @pl.when(k_tile == last_tile)
    def _():
        for h in range(heads):
            o_ref[:, h * HD:(h + 1) * HD] = (acc_sc[h] / l_sc[h]).T.astype(o_ref.dtype)


def side_by_side_body(left_ref, right_ref, out_ref, sems):
    width = left_ref.shape[1]
    first = pltpu.make_async_copy(left_ref, out_ref.at[:, :width], sems.at[0])
    second = pltpu.make_async_copy(right_ref, out_ref.at[:, width:], sems.at[1])
    first.start()
    second.start()
    first.wait()
    second.wait()


def side_by_side(left, right):
    rows, width = left.shape
    return pl.pallas_call(
        side_by_side_body,
        out_shape=jax.ShapeDtypeStruct((rows, 2 * width), left.dtype),
        in_specs=[pl.BlockSpec(memory_space=pl.ANY), pl.BlockSpec(memory_space=pl.ANY)],
        out_specs=pl.BlockSpec(memory_space=pl.ANY),
        scratch_shapes=[pltpu.SemaphoreType.DMA((2,))],
    )(left, right)


def prompt_attention(queries, block_index, long_k, long_v, early=None):
    row_count, width = queries.shape
    heads_dev = width // HD
    kv_piece = lax.all_gather(side_by_side(long_k, long_v), "blk", axis=0, tiled=True)
    if early is not None:
        kv_piece, early = lax.optimization_barrier((kv_piece, early))
    piece_rows = kv_piece.shape[0]
    block_count = lax.axis_size("blk")
    tq = row_count // 2
    chip_count = block_count // 2
    mirror = [(src, 2 * (chip_count - 1 - src // 2) + src % 2) for src in range(block_count)]
    partner_block = 2 * (chip_count - 1 - block_index // 2) + block_index % 2
    partner_half = lax.ppermute(queries[tq:], "blk", mirror)
    tk = min(piece_rows, 2 * row_count)
    own_first = block_index * row_count
    lent_first = partner_block * row_count + tq
    own_steps = (own_first + tq - 1) // tk + 1
    tile_pos = jnp.stack([own_first, lent_first, own_steps]).astype(jnp.int32)
    counts = {
        (d * row_count + tq - 1) // tk + (dict(mirror)[d] * row_count + 2 * tq - 1) // tk + 2
        for d in range(block_count)
    }
    assert len(counts) == 1
    step_count = counts.pop()

    def kv_map(column):
        def index(step, pos_ref):
            return (tile_of_step(step, pos_ref)[1], column)

        return index

    def q_map(step, pos_ref):
        return (tile_of_step(step, pos_ref)[0], 0)

    body = functools.partial(flash_body, heads=heads_dev, tq=tq, tk=tk)
    result = pl.pallas_call(
        body,
        out_shape=jax.ShapeDtypeStruct((row_count, width), jnp.bfloat16),
        grid_spec=pltpu.PrefetchScalarGridSpec(
            num_scalar_prefetch=1,
            grid=(step_count,),
            in_specs=[
                pl.BlockSpec((tq, width), q_map),
                pl.BlockSpec((tk, width), kv_map(0)),
                pl.BlockSpec((tk, width), kv_map(1)),
            ],
            out_specs=pl.BlockSpec((tq, width), q_map),
            scratch_shapes=[
                pltpu.VMEM((heads_dev, 1, tq), jnp.float32),
                pltpu.VMEM((heads_dev, 1, tq), jnp.float32),
                pltpu.VMEM((heads_dev, HD, tq), jnp.float32),
            ],
        ),
        compiler_params=pltpu.CompilerParams(dimension_semantics=("arbitrary",)),
    )(tile_pos, jnp.concatenate([queries[:tq], partner_half], 0), kv_piece, kv_piece)
    merged = jnp.concatenate([result[:tq], lax.ppermute(result[tq:], "blk", mirror)], 0)
    return merged, early


def pack_attention(
    short_q, short_k, short_v, short_seg, pool_kv, page_table, block_index, block_count
):
    pack_rows, width = short_q.shape
    heads_dev = width // HD
    pool_pages = pool_kv.shape[0]
    page_len = pool_kv.shape[2]
    page_rows = page_table.reshape(block_count, -1)
    entries = page_rows.shape[1]
    capacity = entries // block_count
    owners = page_rows // pool_pages
    places = page_rows % pool_pages
    wanted = owners == block_index
    ranks = jnp.cumsum(wanted.astype(jnp.int32), axis=1) - 1
    picked = wanted[:, :, None] & (
        ranks[:, :, None] == jnp.arange(capacity, dtype=jnp.int32)[None, None, :]
    )
    send_places = jnp.sum(jnp.where(picked, places[:, :, None], 0), axis=1)
    outgoing = pool_kv[send_places.reshape(-1)].reshape(block_count, capacity, 2, page_len, width)
    arrived = lax.all_to_all(outgoing, "blk", split_axis=0, concat_axis=0, tiled=True)
    my_owners = lax.dynamic_index_in_dim(owners, block_index, 0, keepdims=False)
    order = jnp.arange(entries, dtype=jnp.int32)
    before = (my_owners[None, :] == my_owners[:, None]) & (order[None, :] < order[:, None])
    slots = my_owners * capacity + jnp.sum(before.astype(jnp.int32), axis=1)
    fetched = arrived.reshape(block_count * capacity, 2, page_len, width)[slots]
    cache_len = entries * page_len
    key_rows = jnp.concatenate([fetched[:, 0].reshape(cache_len, width), short_k], 0)
    value_rows = jnp.concatenate([fetched[:, 1].reshape(cache_len, width), short_v], 0)
    segment = short_seg[0]
    positions = jnp.arange(pack_rows, dtype=jnp.int32)
    key_seg = jnp.concatenate([jnp.arange(cache_len, dtype=jnp.int32) // (PPS * page_len), segment])
    key_pos = jnp.concatenate([jnp.full((cache_len,), -1, jnp.int32), positions])
    allowed = ((key_seg[None, :] == segment[:, None]) & (key_pos[None, :] <= positions[:, None]))[
        None
    ]
    query_heads = short_q.reshape(pack_rows, heads_dev, HD)
    key_heads = key_rows.reshape(cache_len + pack_rows, heads_dev, HD)
    value_heads = value_rows.reshape(cache_len + pack_rows, heads_dev, HD)
    scores = jnp.einsum(
        "qhd,khd->hqk", query_heads, key_heads, preferred_element_type=jnp.float32
    ) * HD ** (-0.5)
    scores = jnp.where(allowed, scores, very_negative)
    row_max = jnp.max(scores, axis=-1)
    weights = jnp.where(allowed, jnp.exp(scores - row_max[..., None]), 0.0)
    total = jnp.sum(weights, axis=-1)
    numer = jnp.einsum(
        "hqk,khd->hqd",
        weights.astype(jnp.bfloat16),
        value_heads,
        preferred_element_type=jnp.float32,
    )
    merged = numer / total[..., None]
    return merged.transpose(1, 0, 2).reshape(pack_rows, width).astype(jnp.bfloat16)


def per_device(
    long_q, long_k, long_v, short_q, short_k, short_v, short_seg, pool_kv, page_table, w_out
):
    block_count = lax.axis_size("blk")
    block_index = lax.axis_index("blk")
    short_attn = pack_attention(
        short_q, short_k, short_v, short_seg, pool_kv, page_table, block_index, block_count
    )
    short_rows = lax.all_to_all(short_attn, "req", 0, 1, tiled=True)
    short_out = jnp.dot(short_rows, w_out, preferred_element_type=jnp.float32).astype(jnp.bfloat16)
    long_attn, short_out = prompt_attention(long_q, block_index, long_k, long_v, short_out)
    long_rows = lax.all_to_all(long_attn, "req", 0, 1, tiled=True)
    long_out = jnp.dot(long_rows, w_out, preferred_element_type=jnp.float32).astype(jnp.bfloat16)
    return (long_out, short_out)


def solution(mesh):
    placed = (
        P("blk", "req"),
        P("blk", "req"),
        P("blk", "req"),
        P("blk", "req"),
        P("blk", "req"),
        P("blk", "req"),
        P("blk", None),
        P("blk", None, None, "req"),
        P(),
        P(),
    )
    return jax.shard_map(
        per_device,
        mesh=mesh,
        in_specs=placed,
        out_specs=(P(("blk", "req"), None), P(("blk", "req"), None)),
        check_vma=False,
    )
```

```python
import functools
import math

import jax
import jax.numpy as jnp
from jax import lax
from jax.experimental import pallas as pl
from jax.experimental.pallas import tpu as pltpu
from jax.sharding import PartitionSpec as P

HD = 128
PPS = 4


very_negative = -1e30


def tile_of_step(step, pos_ref):
    q_tile = (step >= pos_ref[2]).astype(jnp.int32)
    return q_tile, step - q_tile * pos_ref[2]


def flash_body(pos_ref, q_ref, k_ref, v_ref, o_ref, m_sc, l_sc, acc_sc, *, heads, tq, tk):
    q_tile, k_tile = tile_of_step(pl.program_id(0), pos_ref)
    first_query = pos_ref[q_tile]
    last_tile = (first_query + tq - 1) // tk

    @pl.when(k_tile == 0)
    def _():
        m_sc[...] = jnp.full(m_sc.shape, very_negative, jnp.float32)
        l_sc[...] = jnp.zeros(l_sc.shape, jnp.float32)
        acc_sc[...] = jnp.zeros(acc_sc.shape, jnp.float32)

    def fold(masked):
        for h in range(heads):
            cols = slice(h * HD, (h + 1) * HD)
            scores = lax.dot_general(
                k_ref[:, :, cols].reshape(tk, HD), q_ref[:, cols], (((1,), (1,)), ((), ())),
                preferred_element_type=jnp.float32,
            ) * HD ** (-0.5)
            if masked:
                key_pos = k_tile * tk + lax.broadcasted_iota(jnp.int32, (tk, tq), 0)
                query_pos = first_query + lax.broadcasted_iota(jnp.int32, (tk, tq), 1)
                scores = jnp.where(key_pos <= query_pos, scores, very_negative)
            run_max = m_sc[h]
            new_max = jnp.maximum(run_max, jnp.max(scores, axis=0, keepdims=True))
            weights = jnp.exp(scores - new_max)
            factor = jnp.exp(run_max - new_max)
            l_sc[h] = l_sc[h] * factor + jnp.sum(weights, axis=0, keepdims=True)
            m_sc[h] = new_max
            acc_sc[h] = acc_sc[h] * factor + lax.dot_general(
                v_ref[:, :, cols].reshape(tk, HD), weights.astype(jnp.bfloat16), (((0,), (0,)), ((), ())),
                preferred_element_type=jnp.float32,
            )

    needs_mask = (k_tile + 1) * tk - 1 > first_query

    @pl.when(jnp.logical_not(needs_mask))
    def _():
        fold(False)

    @pl.when(needs_mask)
    def _():
        fold(True)

    @pl.when(k_tile == last_tile)
    def _():
        for h in range(heads):
            o_ref[:, h * HD:(h + 1) * HD] = (acc_sc[h] / l_sc[h]).T.astype(o_ref.dtype)


def prompt_attention(queries, block_index, long_k, long_v, early=None):
    row_count, width = queries.shape
    heads_dev = width // HD
    kv_piece = lax.all_gather(jnp.stack([long_k, long_v]), "blk", axis=0, tiled=True)
    kv_piece = kv_piece.reshape(-1, 2, row_count, width)
    if early is not None:
        kv_piece, early = lax.optimization_barrier((kv_piece, early))
    piece_rows = kv_piece.shape[0] * row_count
    block_count = lax.axis_size("blk")
    tq = row_count // 2
    chip_count = block_count // 2
    mirror = [(src, 2 * (chip_count - 1 - src // 2) + src % 2) for src in range(block_count)]
    partner_block = 2 * (chip_count - 1 - block_index // 2) + block_index % 2
    partner_half = lax.ppermute(queries[tq:], "blk", mirror)
    tk = min(piece_rows, 2 * row_count)
    own_first = block_index * row_count
    lent_first = partner_block * row_count + tq
    own_steps = (own_first + tq - 1) // tk + 1
    tile_pos = jnp.stack([own_first, lent_first, own_steps]).astype(jnp.int32)
    counts = {
        (d * row_count + tq - 1) // tk + (dict(mirror)[d] * row_count + 2 * tq - 1) // tk + 2
        for d in range(block_count)
    }
    assert len(counts) == 1
    step_count = counts.pop()

    def kv_map(column):
        def index(step, pos_ref):
            return (tile_of_step(step, pos_ref)[1], column, 0, 0)

        return index

    def q_map(step, pos_ref):
        return (tile_of_step(step, pos_ref)[0], 0)

    body = functools.partial(flash_body, heads=heads_dev, tq=tq, tk=tk)
    result = pl.pallas_call(
        body,
        out_shape=jax.ShapeDtypeStruct((row_count, width), jnp.bfloat16),
        grid_spec=pltpu.PrefetchScalarGridSpec(
            num_scalar_prefetch=1,
            grid=(step_count,),
            in_specs=[
                pl.BlockSpec((tq, width), q_map),
                pl.BlockSpec((tk // row_count, None, row_count, width), kv_map(0)),
                pl.BlockSpec((tk // row_count, None, row_count, width), kv_map(1)),
            ],
            out_specs=pl.BlockSpec((tq, width), q_map),
            scratch_shapes=[
                pltpu.VMEM((heads_dev, 1, tq), jnp.float32),
                pltpu.VMEM((heads_dev, 1, tq), jnp.float32),
                pltpu.VMEM((heads_dev, HD, tq), jnp.float32),
            ],
        ),
        compiler_params=pltpu.CompilerParams(dimension_semantics=("arbitrary",)),
    )(tile_pos, jnp.concatenate([queries[:tq], partner_half], 0), kv_piece, kv_piece)
    merged = jnp.concatenate([result[:tq], lax.ppermute(result[tq:], "blk", mirror)], 0)
    return merged, early


def pack_attention(
    short_q, short_k, short_v, short_seg, pool_kv, page_table, block_index, block_count
):
    pack_rows, width = short_q.shape
    heads_dev = width // HD
    pool_pages = pool_kv.shape[0]
    page_len = pool_kv.shape[2]
    page_rows = page_table.reshape(block_count, -1)
    entries = page_rows.shape[1]
    capacity = entries // block_count
    owners = page_rows // pool_pages
    places = page_rows % pool_pages
    wanted = owners == block_index
    ranks = jnp.cumsum(wanted.astype(jnp.int32), axis=1) - 1
    picked = wanted[:, :, None] & (
        ranks[:, :, None] == jnp.arange(capacity, dtype=jnp.int32)[None, None, :]
    )
    send_places = jnp.sum(jnp.where(picked, places[:, :, None], 0), axis=1)
    outgoing = pool_kv[send_places.reshape(-1)].reshape(block_count, capacity, 2, page_len, width)
    arrived = lax.all_to_all(outgoing, "blk", split_axis=0, concat_axis=0, tiled=True)
    my_owners = lax.dynamic_index_in_dim(owners, block_index, 0, keepdims=False)
    order = jnp.arange(entries, dtype=jnp.int32)
    before = (my_owners[None, :] == my_owners[:, None]) & (order[None, :] < order[:, None])
    slots = my_owners * capacity + jnp.sum(before.astype(jnp.int32), axis=1)
    fetched = arrived.reshape(block_count * capacity, 2, page_len, width)[slots]
    cache_len = entries * page_len
    key_rows = jnp.concatenate([fetched[:, 0].reshape(cache_len, width), short_k], 0)
    value_rows = jnp.concatenate([fetched[:, 1].reshape(cache_len, width), short_v], 0)
    segment = short_seg[0]
    positions = jnp.arange(pack_rows, dtype=jnp.int32)
    key_seg = jnp.concatenate([jnp.arange(cache_len, dtype=jnp.int32) // (PPS * page_len), segment])
    key_pos = jnp.concatenate([jnp.full((cache_len,), -1, jnp.int32), positions])
    allowed = ((key_seg[None, :] == segment[:, None]) & (key_pos[None, :] <= positions[:, None]))[
        None
    ]
    query_heads = short_q.reshape(pack_rows, heads_dev, HD)
    key_heads = key_rows.reshape(cache_len + pack_rows, heads_dev, HD)
    value_heads = value_rows.reshape(cache_len + pack_rows, heads_dev, HD)
    scores = jnp.einsum(
        "qhd,khd->hqk", query_heads, key_heads, preferred_element_type=jnp.float32
    ) * HD ** (-0.5)
    scores = jnp.where(allowed, scores, very_negative)
    row_max = jnp.max(scores, axis=-1)
    weights = jnp.where(allowed, jnp.exp(scores - row_max[..., None]), 0.0)
    total = jnp.sum(weights, axis=-1)
    numer = jnp.einsum(
        "hqk,khd->hqd",
        weights.astype(jnp.bfloat16),
        value_heads,
        preferred_element_type=jnp.float32,
    )
    merged = numer / total[..., None]
    return merged.transpose(1, 0, 2).reshape(pack_rows, width).astype(jnp.bfloat16)


def per_device(
    long_q, long_k, long_v, short_q, short_k, short_v, short_seg, pool_kv, page_table, w_out
):
    block_count = lax.axis_size("blk")
    block_index = lax.axis_index("blk")
    short_attn = pack_attention(
        short_q, short_k, short_v, short_seg, pool_kv, page_table, block_index, block_count
    )
    short_rows = lax.all_to_all(short_attn, "req", 0, 1, tiled=True)
    short_out = jnp.dot(short_rows, w_out, preferred_element_type=jnp.float32).astype(jnp.bfloat16)
    long_attn, short_out = prompt_attention(long_q, block_index, long_k, long_v, short_out)
    long_rows = lax.all_to_all(long_attn, "req", 0, 1, tiled=True)
    long_out = jnp.dot(long_rows, w_out, preferred_element_type=jnp.float32).astype(jnp.bfloat16)
    return (long_out, short_out)


def solution(mesh):
    placed = (
        P("blk", "req"),
        P("blk", "req"),
        P("blk", "req"),
        P("blk", "req"),
        P("blk", "req"),
        P("blk", "req"),
        P("blk", None),
        P("blk", None, None, "req"),
        P(),
        P(),
    )
    return jax.shard_map(
        per_device,
        mesh=mesh,
        in_specs=placed,
        out_specs=(P(("blk", "req"), None), P(("blk", "req"), None)),
        check_vma=False,
    )
```

```python
import functools
import math

import jax
import jax.numpy as jnp
from jax import lax
from jax.experimental import pallas as pl
from jax.experimental.pallas import tpu as pltpu
from jax.sharding import PartitionSpec as P

HD = 128
PPS = 4


very_negative = -1e30


def tile_of_step(step, pos_ref):
    q_tile = (step >= pos_ref[2]).astype(jnp.int32)
    return q_tile, step - q_tile * pos_ref[2]


def flash_body(pos_ref, q_ref, k_ref, v_ref, own_ref, lent_ref, m_sc, l_sc, acc_sc, *, heads, tq, tk):
    q_tile, k_tile = tile_of_step(pl.program_id(0), pos_ref)
    first_query = pos_ref[q_tile]
    last_tile = (first_query + tq - 1) // tk

    @pl.when(k_tile == 0)
    def _():
        m_sc[...] = jnp.full(m_sc.shape, very_negative, jnp.float32)
        l_sc[...] = jnp.zeros(l_sc.shape, jnp.float32)
        acc_sc[...] = jnp.zeros(acc_sc.shape, jnp.float32)

    def fold(masked):
        for h in range(heads):
            cols = slice(h * HD, (h + 1) * HD)
            scores = lax.dot_general(
                k_ref[:, cols], q_ref[:, cols], (((1,), (1,)), ((), ())),
                preferred_element_type=jnp.float32,
            ) * HD ** (-0.5)
            if masked:
                key_pos = k_tile * tk + lax.broadcasted_iota(jnp.int32, (tk, tq), 0)
                query_pos = first_query + lax.broadcasted_iota(jnp.int32, (tk, tq), 1)
                scores = jnp.where(key_pos <= query_pos, scores, very_negative)
            run_max = m_sc[h]
            new_max = jnp.maximum(run_max, jnp.max(scores, axis=0, keepdims=True))
            weights = jnp.exp(scores - new_max)
            factor = jnp.exp(run_max - new_max)
            l_sc[h] = l_sc[h] * factor + jnp.sum(weights, axis=0, keepdims=True)
            m_sc[h] = new_max
            acc_sc[h] = acc_sc[h] * factor + lax.dot_general(
                v_ref[:, cols], weights.astype(jnp.bfloat16), (((0,), (0,)), ((), ())),
                preferred_element_type=jnp.float32,
            )

    needs_mask = (k_tile + 1) * tk - 1 > first_query

    @pl.when(jnp.logical_not(needs_mask))
    def _():
        fold(False)

    @pl.when(needs_mask)
    def _():
        fold(True)

    for tile, o_ref in ((0, own_ref), (1, lent_ref)):

        @pl.when((k_tile == last_tile) & (q_tile == tile))
        def _():
            for h in range(heads):
                o_ref[:, h * HD:(h + 1) * HD] = (acc_sc[h] / l_sc[h]).T.astype(o_ref.dtype)


def prompt_attention(queries, block_index, long_k, long_v, early=None):
    row_count, width = queries.shape
    heads_dev = width // HD
    kv_piece = lax.all_gather(jnp.concatenate([long_k, long_v], 1), "blk", axis=0, tiled=True)
    if early is not None:
        kv_piece, early = lax.optimization_barrier((kv_piece, early))
    piece_rows = kv_piece.shape[0]
    block_count = lax.axis_size("blk")
    tq = row_count // 2
    chip_count = block_count // 2
    mirror = [(src, 2 * (chip_count - 1 - src // 2) + src % 2) for src in range(block_count)]
    partner_block = 2 * (chip_count - 1 - block_index // 2) + block_index % 2
    partner_half = lax.ppermute(queries[tq:], "blk", mirror)
    tk = min(piece_rows, 2 * row_count)
    own_first = block_index * row_count
    lent_first = partner_block * row_count + tq
    own_steps = (own_first + tq - 1) // tk + 1
    tile_pos = jnp.stack([own_first, lent_first, own_steps]).astype(jnp.int32)
    counts = {
        (d * row_count + tq - 1) // tk + (dict(mirror)[d] * row_count + 2 * tq - 1) // tk + 2
        for d in range(block_count)
    }
    assert len(counts) == 1
    step_count = counts.pop()

    def kv_map(column):
        def index(step, pos_ref):
            return (tile_of_step(step, pos_ref)[1], column)

        return index

    def q_map(step, pos_ref):
        return (tile_of_step(step, pos_ref)[0], 0)

    body = functools.partial(flash_body, heads=heads_dev, tq=tq, tk=tk)
    result = pl.pallas_call(
        body,
        out_shape=(
            jax.ShapeDtypeStruct((tq, width), jnp.bfloat16),
            jax.ShapeDtypeStruct((tq, width), jnp.bfloat16),
        ),
        grid_spec=pltpu.PrefetchScalarGridSpec(
            num_scalar_prefetch=1,
            grid=(step_count,),
            in_specs=[
                pl.BlockSpec((tq, width), q_map),
                pl.BlockSpec((tk, width), kv_map(0)),
                pl.BlockSpec((tk, width), kv_map(1)),
            ],
            out_specs=[
                pl.BlockSpec((tq, width), lambda step, pos_ref: (0, 0)),
                pl.BlockSpec((tq, width), lambda step, pos_ref: (0, 0)),
            ],
            scratch_shapes=[
                pltpu.VMEM((heads_dev, 1, tq), jnp.float32),
                pltpu.VMEM((heads_dev, 1, tq), jnp.float32),
                pltpu.VMEM((heads_dev, HD, tq), jnp.float32),
            ],
        ),
        compiler_params=pltpu.CompilerParams(dimension_semantics=("arbitrary",)),
    )(tile_pos, jnp.concatenate([queries[:tq], partner_half], 0), kv_piece, kv_piece)
    own_rows, lent_rows = result
    merged = jnp.concatenate([own_rows, lax.ppermute(lent_rows, "blk", mirror)], 0)
    return merged, early


def pack_attention(
    short_q, short_k, short_v, short_seg, pool_kv, page_table, block_index, block_count
):
    pack_rows, width = short_q.shape
    heads_dev = width // HD
    pool_pages = pool_kv.shape[0]
    page_len = pool_kv.shape[2]
    page_rows = page_table.reshape(block_count, -1)
    entries = page_rows.shape[1]
    capacity = entries // block_count
    owners = page_rows // pool_pages
    places = page_rows % pool_pages
    wanted = owners == block_index
    ranks = jnp.cumsum(wanted.astype(jnp.int32), axis=1) - 1
    picked = wanted[:, :, None] & (
        ranks[:, :, None] == jnp.arange(capacity, dtype=jnp.int32)[None, None, :]
    )
    send_places = jnp.sum(jnp.where(picked, places[:, :, None], 0), axis=1)
    outgoing = pool_kv[send_places.reshape(-1)].reshape(block_count, capacity, 2, page_len, width)
    arrived = lax.all_to_all(outgoing, "blk", split_axis=0, concat_axis=0, tiled=True)
    my_owners = lax.dynamic_index_in_dim(owners, block_index, 0, keepdims=False)
    order = jnp.arange(entries, dtype=jnp.int32)
    before = (my_owners[None, :] == my_owners[:, None]) & (order[None, :] < order[:, None])
    slots = my_owners * capacity + jnp.sum(before.astype(jnp.int32), axis=1)
    fetched = arrived.reshape(block_count * capacity, 2, page_len, width)[slots]
    cache_len = entries * page_len
    key_rows = jnp.concatenate([fetched[:, 0].reshape(cache_len, width), short_k], 0)
    value_rows = jnp.concatenate([fetched[:, 1].reshape(cache_len, width), short_v], 0)
    segment = short_seg[0]
    positions = jnp.arange(pack_rows, dtype=jnp.int32)
    key_seg = jnp.concatenate([jnp.arange(cache_len, dtype=jnp.int32) // (PPS * page_len), segment])
    key_pos = jnp.concatenate([jnp.full((cache_len,), -1, jnp.int32), positions])
    allowed = ((key_seg[None, :] == segment[:, None]) & (key_pos[None, :] <= positions[:, None]))[
        None
    ]
    query_heads = short_q.reshape(pack_rows, heads_dev, HD)
    key_heads = key_rows.reshape(cache_len + pack_rows, heads_dev, HD)
    value_heads = value_rows.reshape(cache_len + pack_rows, heads_dev, HD)
    scores = jnp.einsum(
        "qhd,khd->hqk", query_heads, key_heads, preferred_element_type=jnp.float32
    ) * HD ** (-0.5)
    scores = jnp.where(allowed, scores, very_negative)
    row_max = jnp.max(scores, axis=-1)
    weights = jnp.where(allowed, jnp.exp(scores - row_max[..., None]), 0.0)
    total = jnp.sum(weights, axis=-1)
    numer = jnp.einsum(
        "hqk,khd->hqd",
        weights.astype(jnp.bfloat16),
        value_heads,
        preferred_element_type=jnp.float32,
    )
    merged = numer / total[..., None]
    return merged.transpose(1, 0, 2).reshape(pack_rows, width).astype(jnp.bfloat16)


def per_device(
    long_q, long_k, long_v, short_q, short_k, short_v, short_seg, pool_kv, page_table, w_out
):
    block_count = lax.axis_size("blk")
    block_index = lax.axis_index("blk")
    short_attn = pack_attention(
        short_q, short_k, short_v, short_seg, pool_kv, page_table, block_index, block_count
    )
    short_rows = lax.all_to_all(short_attn, "req", 0, 1, tiled=True)
    short_out = jnp.dot(short_rows, w_out, preferred_element_type=jnp.float32).astype(jnp.bfloat16)
    long_attn, short_out = prompt_attention(long_q, block_index, long_k, long_v, short_out)
    long_rows = lax.all_to_all(long_attn, "req", 0, 1, tiled=True)
    long_out = jnp.dot(long_rows, w_out, preferred_element_type=jnp.float32).astype(jnp.bfloat16)
    return (long_out, short_out)


def solution(mesh):
    placed = (
        P("blk", "req"),
        P("blk", "req"),
        P("blk", "req"),
        P("blk", "req"),
        P("blk", "req"),
        P("blk", "req"),
        P("blk", None),
        P("blk", None, None, "req"),
        P(),
        P(),
    )
    return jax.shard_map(
        per_device,
        mesh=mesh,
        in_specs=placed,
        out_specs=(P(("blk", "req"), None), P(("blk", "req"), None)),
        check_vma=False,
    )
```

```python
import functools
import math

import jax
import jax.numpy as jnp
from jax import lax
from jax.experimental import pallas as pl
from jax.experimental.pallas import tpu as pltpu
from jax.sharding import PartitionSpec as P

HD = 128
PPS = 4


very_negative = -1e30


def tile_of_step(step, pos_ref):
    q_tile = (step >= pos_ref[2]).astype(jnp.int32)
    return q_tile, step - q_tile * pos_ref[2]


def flash_body(pos_ref, q_ref, k_ref, v_ref, o_ref, m_sc, l_sc, acc_sc, *, heads, tq, tk):
    q_tile, k_tile = tile_of_step(pl.program_id(0), pos_ref)
    first_query = pos_ref[q_tile]
    last_tile = (first_query + tq - 1) // tk

    @pl.when(k_tile == 0)
    def _():
        m_sc[...] = jnp.full(m_sc.shape, very_negative, jnp.float32)
        l_sc[...] = jnp.zeros(l_sc.shape, jnp.float32)
        acc_sc[...] = jnp.zeros(acc_sc.shape, jnp.float32)

    def fold(masked):
        for h in range(heads):
            cols = slice(h * HD, (h + 1) * HD)
            scores = lax.dot_general(
                k_ref[:, cols], q_ref[:, cols], (((1,), (1,)), ((), ())),
                preferred_element_type=jnp.float32,
            ) * HD ** (-0.5)
            if masked:
                key_pos = k_tile * tk + lax.broadcasted_iota(jnp.int32, (tk, tq), 0)
                query_pos = first_query + lax.broadcasted_iota(jnp.int32, (tk, tq), 1)
                scores = jnp.where(key_pos <= query_pos, scores, very_negative)
            run_max = m_sc[h]
            new_max = jnp.maximum(run_max, jnp.max(scores, axis=0, keepdims=True))
            weights = jnp.exp(scores - new_max)
            factor = jnp.exp(run_max - new_max)
            l_sc[h] = l_sc[h] * factor + jnp.sum(weights, axis=0, keepdims=True)
            m_sc[h] = new_max
            acc_sc[h] = acc_sc[h] * factor + lax.dot_general(
                v_ref[:, cols], weights.astype(jnp.bfloat16), (((0,), (0,)), ((), ())),
                preferred_element_type=jnp.float32,
            )

    needs_mask = (k_tile + 1) * tk - 1 > first_query

    @pl.when(jnp.logical_not(needs_mask))
    def _():
        fold(False)

    @pl.when(needs_mask)
    def _():
        fold(True)

    @pl.when(k_tile == last_tile)
    def _():
        for h in range(heads):
            o_ref[:, h * HD:(h + 1) * HD] = (acc_sc[h] / l_sc[h]).T.astype(o_ref.dtype)


def prompt_attention(queries, block_index, long_k, long_v, early=None):
    row_count, width = queries.shape
    heads_dev = width // HD
    block_count = lax.axis_size("blk")
    tq = row_count // 2
    chip_count = block_count // 2
    mirror = [(src, 2 * (chip_count - 1 - src // 2) + src % 2) for src in range(block_count)]
    partner_block = 2 * (chip_count - 1 - block_index // 2) + block_index % 2
    partner_half = lax.ppermute(queries[tq:], "blk", mirror)
    own_kv, partner_half = lax.optimization_barrier(
        (jnp.concatenate([long_k, long_v], 1), partner_half)
    )
    kv_piece = lax.all_gather(own_kv, "blk", axis=0, tiled=True)
    if early is not None:
        kv_piece, early = lax.optimization_barrier((kv_piece, early))
    piece_rows = kv_piece.shape[0]
    tk = min(piece_rows, 2 * row_count)
    own_first = block_index * row_count
    lent_first = partner_block * row_count + tq
    own_steps = (own_first + tq - 1) // tk + 1
    tile_pos = jnp.stack([own_first, lent_first, own_steps]).astype(jnp.int32)
    counts = {
        (d * row_count + tq - 1) // tk + (dict(mirror)[d] * row_count + 2 * tq - 1) // tk + 2
        for d in range(block_count)
    }
    assert len(counts) == 1
    step_count = counts.pop()

    def kv_map(column):
        def index(step, pos_ref):
            return (tile_of_step(step, pos_ref)[1], column)

        return index

    def q_map(step, pos_ref):
        return (tile_of_step(step, pos_ref)[0], 0)

    body = functools.partial(flash_body, heads=heads_dev, tq=tq, tk=tk)
    result = pl.pallas_call(
        body,
        out_shape=jax.ShapeDtypeStruct((row_count, width), jnp.bfloat16),
        grid_spec=pltpu.PrefetchScalarGridSpec(
            num_scalar_prefetch=1,
            grid=(step_count,),
            in_specs=[
                pl.BlockSpec((tq, width), q_map),
                pl.BlockSpec((tk, width), kv_map(0)),
                pl.BlockSpec((tk, width), kv_map(1)),
            ],
            out_specs=pl.BlockSpec((tq, width), q_map),
            scratch_shapes=[
                pltpu.VMEM((heads_dev, 1, tq), jnp.float32),
                pltpu.VMEM((heads_dev, 1, tq), jnp.float32),
                pltpu.VMEM((heads_dev, HD, tq), jnp.float32),
            ],
        ),
        compiler_params=pltpu.CompilerParams(dimension_semantics=("arbitrary",)),
    )(tile_pos, jnp.concatenate([queries[:tq], partner_half], 0), kv_piece, kv_piece)
    merged = jnp.concatenate([result[:tq], lax.ppermute(result[tq:], "blk", mirror)], 0)
    return merged, early


def pack_attention(
    short_q, short_k, short_v, short_seg, pool_kv, page_table, block_index, block_count
):
    pack_rows, width = short_q.shape
    heads_dev = width // HD
    pool_pages = pool_kv.shape[0]
    page_len = pool_kv.shape[2]
    page_rows = page_table.reshape(block_count, -1)
    entries = page_rows.shape[1]
    capacity = entries // block_count
    owners = page_rows // pool_pages
    places = page_rows % pool_pages
    wanted = owners == block_index
    ranks = jnp.cumsum(wanted.astype(jnp.int32), axis=1) - 1
    picked = wanted[:, :, None] & (
        ranks[:, :, None] == jnp.arange(capacity, dtype=jnp.int32)[None, None, :]
    )
    send_places = jnp.sum(jnp.where(picked, places[:, :, None], 0), axis=1)
    outgoing = pool_kv[send_places.reshape(-1)].reshape(block_count, capacity, 2, page_len, width)
    arrived = lax.all_to_all(outgoing, "blk", split_axis=0, concat_axis=0, tiled=True)
    my_owners = lax.dynamic_index_in_dim(owners, block_index, 0, keepdims=False)
    order = jnp.arange(entries, dtype=jnp.int32)
    before = (my_owners[None, :] == my_owners[:, None]) & (order[None, :] < order[:, None])
    slots = my_owners * capacity + jnp.sum(before.astype(jnp.int32), axis=1)
    fetched = arrived.reshape(block_count * capacity, 2, page_len, width)[slots]
    cache_len = entries * page_len
    key_rows = jnp.concatenate([fetched[:, 0].reshape(cache_len, width), short_k], 0)
    value_rows = jnp.concatenate([fetched[:, 1].reshape(cache_len, width), short_v], 0)
    segment = short_seg[0]
    positions = jnp.arange(pack_rows, dtype=jnp.int32)
    key_seg = jnp.concatenate([jnp.arange(cache_len, dtype=jnp.int32) // (PPS * page_len), segment])
    key_pos = jnp.concatenate([jnp.full((cache_len,), -1, jnp.int32), positions])
    allowed = ((key_seg[None, :] == segment[:, None]) & (key_pos[None, :] <= positions[:, None]))[
        None
    ]
    query_heads = short_q.reshape(pack_rows, heads_dev, HD)
    key_heads = key_rows.reshape(cache_len + pack_rows, heads_dev, HD)
    value_heads = value_rows.reshape(cache_len + pack_rows, heads_dev, HD)
    scores = jnp.einsum(
        "qhd,khd->hqk", query_heads, key_heads, preferred_element_type=jnp.float32
    ) * HD ** (-0.5)
    scores = jnp.where(allowed, scores, very_negative)
    row_max = jnp.max(scores, axis=-1)
    weights = jnp.where(allowed, jnp.exp(scores - row_max[..., None]), 0.0)
    total = jnp.sum(weights, axis=-1)
    numer = jnp.einsum(
        "hqk,khd->hqd",
        weights.astype(jnp.bfloat16),
        value_heads,
        preferred_element_type=jnp.float32,
    )
    merged = numer / total[..., None]
    return merged.transpose(1, 0, 2).reshape(pack_rows, width).astype(jnp.bfloat16)


def per_device(
    long_q, long_k, long_v, short_q, short_k, short_v, short_seg, pool_kv, page_table, w_out
):
    block_count = lax.axis_size("blk")
    block_index = lax.axis_index("blk")
    short_attn = pack_attention(
        short_q, short_k, short_v, short_seg, pool_kv, page_table, block_index, block_count
    )
    short_rows = lax.all_to_all(short_attn, "req", 0, 1, tiled=True)
    short_out = jnp.dot(short_rows, w_out, preferred_element_type=jnp.float32).astype(jnp.bfloat16)
    long_attn, short_out = prompt_attention(long_q, block_index, long_k, long_v, short_out)
    long_rows = lax.all_to_all(long_attn, "req", 0, 1, tiled=True)
    long_out = jnp.dot(long_rows, w_out, preferred_element_type=jnp.float32).astype(jnp.bfloat16)
    return (long_out, short_out)


def solution(mesh):
    placed = (
        P("blk", "req"),
        P("blk", "req"),
        P("blk", "req"),
        P("blk", "req"),
        P("blk", "req"),
        P("blk", "req"),
        P("blk", None),
        P("blk", None, None, "req"),
        P(),
        P(),
    )
    return jax.shard_map(
        per_device,
        mesh=mesh,
        in_specs=placed,
        out_specs=(P(("blk", "req"), None), P(("blk", "req"), None)),
        check_vma=False,
    )
```

```python
import functools
import math

import jax
import jax.numpy as jnp
from jax import lax
from jax.experimental import pallas as pl
from jax.experimental.pallas import tpu as pltpu
from jax.sharding import PartitionSpec as P

HD = 128
PPS = 4


very_negative = -1e30


def tile_of_step(step, pos_ref):
    q_tile = (step >= pos_ref[2]).astype(jnp.int32)
    return q_tile, step - q_tile * pos_ref[2]


def flash_body(pos_ref, q_ref, k_ref, v_ref, o_ref, m_sc, l_sc, acc_sc, *, heads, tq, tk):
    q_tile, k_tile = tile_of_step(pl.program_id(0), pos_ref)
    first_query = pos_ref[q_tile]
    last_tile = (first_query + tq - 1) // tk

    @pl.when(k_tile == 0)
    def _():
        m_sc[...] = jnp.full(m_sc.shape, very_negative, jnp.float32)
        l_sc[...] = jnp.zeros(l_sc.shape, jnp.float32)
        acc_sc[...] = jnp.zeros(acc_sc.shape, jnp.float32)

    def fold(masked, keys=tk):
        for h in range(heads):
            cols = slice(h * HD, (h + 1) * HD)
            scores = lax.dot_general(
                k_ref[:keys, cols], q_ref[:, cols], (((1,), (1,)), ((), ())),
                preferred_element_type=jnp.float32,
            ) * HD ** (-0.5)
            if masked:
                key_pos = k_tile * tk + lax.broadcasted_iota(jnp.int32, (keys, tq), 0)
                query_pos = first_query + lax.broadcasted_iota(jnp.int32, (keys, tq), 1)
                scores = jnp.where(key_pos <= query_pos, scores, very_negative)
            run_max = m_sc[h]
            new_max = jnp.maximum(run_max, jnp.max(scores, axis=0, keepdims=True))
            weights = jnp.exp(scores - new_max)
            factor = jnp.exp(run_max - new_max)
            l_sc[h] = l_sc[h] * factor + jnp.sum(weights, axis=0, keepdims=True)
            m_sc[h] = new_max
            acc_sc[h] = acc_sc[h] * factor + lax.dot_general(
                v_ref[:keys, cols], weights.astype(jnp.bfloat16), (((0,), (0,)), ((), ())),
                preferred_element_type=jnp.float32,
            )

    needs_mask = (k_tile + 1) * tk - 1 > first_query

    @pl.when(jnp.logical_not(needs_mask))
    def _():
        fold(False)

    half_only = k_tile * tk + tk // 2 > first_query + tq - 1

    @pl.when(needs_mask & half_only)
    def _():
        fold(True, tk // 2)

    @pl.when(needs_mask & jnp.logical_not(half_only))
    def _():
        fold(True)

    @pl.when(k_tile == last_tile)
    def _():
        for h in range(heads):
            o_ref[:, h * HD:(h + 1) * HD] = (acc_sc[h] / l_sc[h]).T.astype(o_ref.dtype)


def prompt_attention(queries, block_index, long_k, long_v, early=None):
    row_count, width = queries.shape
    heads_dev = width // HD
    kv_piece = lax.all_gather(jnp.concatenate([long_k, long_v], 1), "blk", axis=0, tiled=True)
    if early is not None:
        kv_piece, early = lax.optimization_barrier((kv_piece, early))
    piece_rows = kv_piece.shape[0]
    block_count = lax.axis_size("blk")
    tq = row_count // 2
    mirror = [(src, block_count - 1 - src) for src in range(block_count)]
    partner_half = lax.ppermute(queries[tq:], "blk", mirror)
    tk = min(piece_rows, 2 * row_count)
    own_first = block_index * row_count
    lent_first = (block_count - 1 - block_index) * row_count + tq
    own_steps = (own_first + tq - 1) // tk + 1
    tile_pos = jnp.stack([own_first, lent_first, own_steps]).astype(jnp.int32)
    counts = {
        (d * row_count + tq - 1) // tk + ((block_count - 1 - d) * row_count + 2 * tq - 1) // tk + 2
        for d in range(block_count)
    }
    assert len(counts) == 1
    step_count = counts.pop()

    def kv_map(column):
        def index(step, pos_ref):
            return (tile_of_step(step, pos_ref)[1], column)

        return index

    def q_map(step, pos_ref):
        return (tile_of_step(step, pos_ref)[0], 0)

    body = functools.partial(flash_body, heads=heads_dev, tq=tq, tk=tk)
    result = pl.pallas_call(
        body,
        out_shape=jax.ShapeDtypeStruct((row_count, width), jnp.bfloat16),
        grid_spec=pltpu.PrefetchScalarGridSpec(
            num_scalar_prefetch=1,
            grid=(step_count,),
            in_specs=[
                pl.BlockSpec((tq, width), q_map),
                pl.BlockSpec((tk, width), kv_map(0)),
                pl.BlockSpec((tk, width), kv_map(1)),
            ],
            out_specs=pl.BlockSpec((tq, width), q_map),
            scratch_shapes=[
                pltpu.VMEM((heads_dev, 1, tq), jnp.float32),
                pltpu.VMEM((heads_dev, 1, tq), jnp.float32),
                pltpu.VMEM((heads_dev, HD, tq), jnp.float32),
            ],
        ),
        compiler_params=pltpu.CompilerParams(dimension_semantics=("arbitrary",)),
    )(tile_pos, jnp.concatenate([queries[:tq], partner_half], 0), kv_piece, kv_piece)
    merged = jnp.concatenate([result[:tq], lax.ppermute(result[tq:], "blk", mirror)], 0)
    return merged, early


def pack_attention(
    short_q, short_k, short_v, short_seg, pool_kv, page_table, block_index, block_count
):
    pack_rows, width = short_q.shape
    heads_dev = width // HD
    pool_pages = pool_kv.shape[0]
    page_len = pool_kv.shape[2]
    page_rows = page_table.reshape(block_count, -1)
    entries = page_rows.shape[1]
    capacity = entries // block_count
    owners = page_rows // pool_pages
    places = page_rows % pool_pages
    wanted = owners == block_index
    ranks = jnp.cumsum(wanted.astype(jnp.int32), axis=1) - 1
    picked = wanted[:, :, None] & (
        ranks[:, :, None] == jnp.arange(capacity, dtype=jnp.int32)[None, None, :]
    )
    send_places = jnp.sum(jnp.where(picked, places[:, :, None], 0), axis=1)
    outgoing = pool_kv[send_places.reshape(-1)].reshape(block_count, capacity, 2, page_len, width)
    arrived = lax.all_to_all(outgoing, "blk", split_axis=0, concat_axis=0, tiled=True)
    my_owners = lax.dynamic_index_in_dim(owners, block_index, 0, keepdims=False)
    order = jnp.arange(entries, dtype=jnp.int32)
    before = (my_owners[None, :] == my_owners[:, None]) & (order[None, :] < order[:, None])
    slots = my_owners * capacity + jnp.sum(before.astype(jnp.int32), axis=1)
    fetched = arrived.reshape(block_count * capacity, 2, page_len, width)[slots]
    cache_len = entries * page_len
    key_rows = jnp.concatenate([fetched[:, 0].reshape(cache_len, width), short_k], 0)
    value_rows = jnp.concatenate([fetched[:, 1].reshape(cache_len, width), short_v], 0)
    segment = short_seg[0]
    positions = jnp.arange(pack_rows, dtype=jnp.int32)
    key_seg = jnp.concatenate([jnp.arange(cache_len, dtype=jnp.int32) // (PPS * page_len), segment])
    key_pos = jnp.concatenate([jnp.full((cache_len,), -1, jnp.int32), positions])
    allowed = ((key_seg[None, :] == segment[:, None]) & (key_pos[None, :] <= positions[:, None]))[
        None
    ]
    query_heads = short_q.reshape(pack_rows, heads_dev, HD)
    key_heads = key_rows.reshape(cache_len + pack_rows, heads_dev, HD)
    value_heads = value_rows.reshape(cache_len + pack_rows, heads_dev, HD)
    scores = jnp.einsum(
        "qhd,khd->hqk", query_heads, key_heads, preferred_element_type=jnp.float32
    ) * HD ** (-0.5)
    scores = jnp.where(allowed, scores, very_negative)
    row_max = jnp.max(scores, axis=-1)
    weights = jnp.where(allowed, jnp.exp(scores - row_max[..., None]), 0.0)
    total = jnp.sum(weights, axis=-1)
    numer = jnp.einsum(
        "hqk,khd->hqd",
        weights.astype(jnp.bfloat16),
        value_heads,
        preferred_element_type=jnp.float32,
    )
    merged = numer / total[..., None]
    return merged.transpose(1, 0, 2).reshape(pack_rows, width).astype(jnp.bfloat16)


def per_device(
    long_q, long_k, long_v, short_q, short_k, short_v, short_seg, pool_kv, page_table, w_out
):
    block_count = lax.axis_size("blk")
    block_index = lax.axis_index("blk")
    short_attn = pack_attention(
        short_q, short_k, short_v, short_seg, pool_kv, page_table, block_index, block_count
    )
    short_rows = lax.all_to_all(short_attn, "req", 0, 1, tiled=True)
    short_out = jnp.dot(short_rows, w_out, preferred_element_type=jnp.float32).astype(jnp.bfloat16)
    long_attn, short_out = prompt_attention(long_q, block_index, long_k, long_v, short_out)
    long_rows = lax.all_to_all(long_attn, "req", 0, 1, tiled=True)
    long_out = jnp.dot(long_rows, w_out, preferred_element_type=jnp.float32).astype(jnp.bfloat16)
    return (long_out, short_out)


def solution(mesh):
    placed = (
        P("blk", "req"),
        P("blk", "req"),
        P("blk", "req"),
        P("blk", "req"),
        P("blk", "req"),
        P("blk", "req"),
        P("blk", None),
        P("blk", None, None, "req"),
        P(),
        P(),
    )
    return jax.shard_map(
        per_device,
        mesh=mesh,
        in_specs=placed,
        out_specs=(P(("blk", "req"), None), P(("blk", "req"), None)),
        check_vma=False,
    )
```

```python
import functools
import math

import jax
import jax.numpy as jnp
from jax import lax
from jax.experimental import pallas as pl
from jax.experimental.pallas import tpu as pltpu
from jax.sharding import PartitionSpec as P

HD = 128
PPS = 4


very_negative = -1e30


def tile_of_step(step, pos_ref):
    q_tile = (step >= pos_ref[2]).astype(jnp.int32)
    return q_tile, step - q_tile * pos_ref[2]


def flash_body(pos_ref, q_ref, k_ref, v_ref, own_ref, lent_ref, m_sc, l_sc, acc_sc, *, heads, tq, tk):
    q_tile, k_tile = tile_of_step(pl.program_id(0), pos_ref)
    first_query = pos_ref[q_tile]
    last_tile = (first_query + tq - 1) // tk

    @pl.when(k_tile == 0)
    def _():
        m_sc[...] = jnp.full(m_sc.shape, very_negative, jnp.float32)
        l_sc[...] = jnp.zeros(l_sc.shape, jnp.float32)
        acc_sc[...] = jnp.zeros(acc_sc.shape, jnp.float32)

    def fold(masked, keys=tk):
        for h in range(heads):
            cols = slice(h * HD, (h + 1) * HD)
            scores = lax.dot_general(
                k_ref[:keys, cols], q_ref[:, cols], (((1,), (1,)), ((), ())),
                preferred_element_type=jnp.float32,
            ) * HD ** (-0.5)
            if masked:
                key_pos = k_tile * tk + lax.broadcasted_iota(jnp.int32, (keys, tq), 0)
                query_pos = first_query + lax.broadcasted_iota(jnp.int32, (keys, tq), 1)
                scores = jnp.where(key_pos <= query_pos, scores, very_negative)
            run_max = m_sc[h]
            new_max = jnp.maximum(run_max, jnp.max(scores, axis=0, keepdims=True))
            weights = jnp.exp(scores - new_max)
            factor = jnp.exp(run_max - new_max)
            l_sc[h] = l_sc[h] * factor + jnp.sum(weights, axis=0, keepdims=True)
            m_sc[h] = new_max
            acc_sc[h] = acc_sc[h] * factor + lax.dot_general(
                v_ref[:keys, cols], weights.astype(jnp.bfloat16), (((0,), (0,)), ((), ())),
                preferred_element_type=jnp.float32,
            )

    needs_mask = (k_tile + 1) * tk - 1 > first_query

    @pl.when(jnp.logical_not(needs_mask))
    def _():
        fold(False)

    half_only = k_tile * tk + tk // 2 > first_query + tq - 1

    @pl.when(needs_mask & half_only)
    def _():
        fold(True, tk // 2)

    @pl.when(needs_mask & jnp.logical_not(half_only))
    def _():
        fold(True)

    for tile, o_ref in ((0, own_ref), (1, lent_ref)):

        @pl.when((k_tile == last_tile) & (q_tile == tile))
        def _():
            for h in range(heads):
                o_ref[:, h * HD:(h + 1) * HD] = (acc_sc[h] / l_sc[h]).T.astype(o_ref.dtype)


def prompt_attention(queries, block_index, long_k, long_v, early=None):
    row_count, width = queries.shape
    heads_dev = width // HD
    kv_piece = lax.all_gather(jnp.concatenate([long_k, long_v], 1), "blk", axis=0, tiled=True)
    if early is not None:
        kv_piece, early = lax.optimization_barrier((kv_piece, early))
    piece_rows = kv_piece.shape[0]
    block_count = lax.axis_size("blk")
    tq = row_count // 2
    mirror = [(src, block_count - 1 - src) for src in range(block_count)]
    partner_half = lax.ppermute(queries[tq:], "blk", mirror)
    tk = min(piece_rows, 2 * row_count)
    own_first = block_index * row_count
    lent_first = (block_count - 1 - block_index) * row_count + tq
    own_steps = (own_first + tq - 1) // tk + 1
    tile_pos = jnp.stack([own_first, lent_first, own_steps]).astype(jnp.int32)
    counts = {
        (d * row_count + tq - 1) // tk + ((block_count - 1 - d) * row_count + 2 * tq - 1) // tk + 2
        for d in range(block_count)
    }
    assert len(counts) == 1
    step_count = counts.pop()

    def kv_map(column):
        def index(step, pos_ref):
            return (tile_of_step(step, pos_ref)[1], column)

        return index

    def q_map(step, pos_ref):
        return (tile_of_step(step, pos_ref)[0], 0)

    body = functools.partial(flash_body, heads=heads_dev, tq=tq, tk=tk)
    result = pl.pallas_call(
        body,
        out_shape=(
            jax.ShapeDtypeStruct((tq, width), jnp.bfloat16),
            jax.ShapeDtypeStruct((tq, width), jnp.bfloat16),
        ),
        grid_spec=pltpu.PrefetchScalarGridSpec(
            num_scalar_prefetch=1,
            grid=(step_count,),
            in_specs=[
                pl.BlockSpec((tq, width), q_map),
                pl.BlockSpec((tk, width), kv_map(0)),
                pl.BlockSpec((tk, width), kv_map(1)),
            ],
            out_specs=[
                pl.BlockSpec((tq, width), lambda step, pos_ref: (0, 0)),
                pl.BlockSpec((tq, width), lambda step, pos_ref: (0, 0)),
            ],
            scratch_shapes=[
                pltpu.VMEM((heads_dev, 1, tq), jnp.float32),
                pltpu.VMEM((heads_dev, 1, tq), jnp.float32),
                pltpu.VMEM((heads_dev, HD, tq), jnp.float32),
            ],
        ),
        compiler_params=pltpu.CompilerParams(dimension_semantics=("arbitrary",)),
    )(tile_pos, jnp.concatenate([queries[:tq], partner_half], 0), kv_piece, kv_piece)
    own_rows, lent_rows = result
    merged = jnp.concatenate([own_rows, lax.ppermute(lent_rows, "blk", mirror)], 0)
    return merged, early


def pack_attention(
    short_q, short_k, short_v, short_seg, pool_kv, page_table, block_index, block_count
):
    pack_rows, width = short_q.shape
    heads_dev = width // HD
    pool_pages = pool_kv.shape[0]
    page_len = pool_kv.shape[2]
    page_rows = page_table.reshape(block_count, -1)
    entries = page_rows.shape[1]
    capacity = entries // block_count
    owners = page_rows // pool_pages
    places = page_rows % pool_pages
    wanted = owners == block_index
    ranks = jnp.cumsum(wanted.astype(jnp.int32), axis=1) - 1
    picked = wanted[:, :, None] & (
        ranks[:, :, None] == jnp.arange(capacity, dtype=jnp.int32)[None, None, :]
    )
    send_places = jnp.sum(jnp.where(picked, places[:, :, None], 0), axis=1)
    outgoing = pool_kv[send_places.reshape(-1)].reshape(block_count, capacity, 2, page_len, width)
    arrived = lax.all_to_all(outgoing, "blk", split_axis=0, concat_axis=0, tiled=True)
    my_owners = lax.dynamic_index_in_dim(owners, block_index, 0, keepdims=False)
    order = jnp.arange(entries, dtype=jnp.int32)
    before = (my_owners[None, :] == my_owners[:, None]) & (order[None, :] < order[:, None])
    slots = my_owners * capacity + jnp.sum(before.astype(jnp.int32), axis=1)
    fetched = arrived.reshape(block_count * capacity, 2, page_len, width)[slots]
    cache_len = entries * page_len
    key_rows = jnp.concatenate([fetched[:, 0].reshape(cache_len, width), short_k], 0)
    value_rows = jnp.concatenate([fetched[:, 1].reshape(cache_len, width), short_v], 0)
    segment = short_seg[0]
    positions = jnp.arange(pack_rows, dtype=jnp.int32)
    key_seg = jnp.concatenate([jnp.arange(cache_len, dtype=jnp.int32) // (PPS * page_len), segment])
    key_pos = jnp.concatenate([jnp.full((cache_len,), -1, jnp.int32), positions])
    allowed = ((key_seg[None, :] == segment[:, None]) & (key_pos[None, :] <= positions[:, None]))[
        None
    ]
    query_heads = short_q.reshape(pack_rows, heads_dev, HD)
    key_heads = key_rows.reshape(cache_len + pack_rows, heads_dev, HD)
    value_heads = value_rows.reshape(cache_len + pack_rows, heads_dev, HD)
    scores = jnp.einsum(
        "qhd,khd->hqk", query_heads, key_heads, preferred_element_type=jnp.float32
    ) * HD ** (-0.5)
    scores = jnp.where(allowed, scores, very_negative)
    row_max = jnp.max(scores, axis=-1)
    weights = jnp.where(allowed, jnp.exp(scores - row_max[..., None]), 0.0)
    total = jnp.sum(weights, axis=-1)
    numer = jnp.einsum(
        "hqk,khd->hqd",
        weights.astype(jnp.bfloat16),
        value_heads,
        preferred_element_type=jnp.float32,
    )
    merged = numer / total[..., None]
    return merged.transpose(1, 0, 2).reshape(pack_rows, width).astype(jnp.bfloat16)


def per_device(
    long_q, long_k, long_v, short_q, short_k, short_v, short_seg, pool_kv, page_table, w_out
):
    block_count = lax.axis_size("blk")
    block_index = lax.axis_index("blk")
    short_attn = pack_attention(
        short_q, short_k, short_v, short_seg, pool_kv, page_table, block_index, block_count
    )
    short_rows = lax.all_to_all(short_attn, "req", 0, 1, tiled=True)
    short_out = jnp.dot(short_rows, w_out, preferred_element_type=jnp.float32).astype(jnp.bfloat16)
    long_attn, short_out = prompt_attention(long_q, block_index, long_k, long_v, short_out)
    long_rows = lax.all_to_all(long_attn, "req", 0, 1, tiled=True)
    long_out = jnp.dot(long_rows, w_out, preferred_element_type=jnp.float32).astype(jnp.bfloat16)
    return (long_out, short_out)


def solution(mesh):
    placed = (
        P("blk", "req"),
        P("blk", "req"),
        P("blk", "req"),
        P("blk", "req"),
        P("blk", "req"),
        P("blk", "req"),
        P("blk", None),
        P("blk", None, None, "req"),
        P(),
        P(),
    )
    return jax.shard_map(
        per_device,
        mesh=mesh,
        in_specs=placed,
        out_specs=(P(("blk", "req"), None), P(("blk", "req"), None)),
        check_vma=False,
    )
```
